32 devices in a mesh: block: 8 (over y, x, core), tm: 4 (over z).
Axes of the slice: x: 2, y: 2, z: 4, core: 2. Of those that a mesh axis runs over, the one named last changes fastest.
Arguments:
- traces: bfloat16 [2048, 8, 6, 1024], P('block', 'tm')
- valid: int32 [2048, 8, 6], P('block', 'tm'), may hold values from 0 to 1, as said below
- panel_owner: int32 [4], replicated, may hold values from 0 to 7, as said below
- panel_start: int32 [4], replicated, may hold values from 0 to 252, as said below
Outputs:
- xcorr: float32 [16, 2048, 1024], P('tm', 'block')
The draws below stay inside these ranges and needn't reach their ends.
Inputs may be any that keep to these rules, and one draw needn't show every extreme that they name: Within one block-tm cell (256 channels by 2 windows by 6 segments) at least an eighth of the segments are valid. `panel_owner`: the panels lie on distinct blocks. `panel_start`: multiples of 4.
All inputs are finite; a program needn't handle non-finite values.
Results may differ from the reference program's by a relative error of at most 0.0051.
Values may be sent and summed in bfloat16 or wider, within the bound.
No kernel may reach another device: no remote copies, remote signals or barrier semaphores. Data moves between devices by JAX's collectives and lax.ppermute only.
A program may use at most 128 MiB of HBM per device.

```python
import math
import jax
import jax.numpy as jnp
from jax import lax

CB = 256
C = 2048
WD = 2
WINDOWS = 8
S = 6
L = 1024
F = 512
PP = 4
NP = 4
P_SIZE = 16
SEGS_DEV = 3072
CAP = 1536


def draw_traces(key, part):
    noise_key, shared_key, scale_key = jax.random.split(key, 3)
    noise_part = jax.random.normal(noise_key, (C, WINDOWS, S, L), jnp.float32)
    shared_weight = 0.15
    lowest = 0.2
    highest = 5.0
    shared = jax.random.normal(shared_key, (WINDOWS, S, L), jnp.float32)
    row_scale = jnp.exp(jax.random.uniform(scale_key, (C, WINDOWS, S, 1), jnp.float32, math.log(lowest), math.log(highest)))
    return (row_scale * (noise_part + shared_weight * shared[None])).astype(jnp.bfloat16)


def draw_valid(key, part):
    block_count = C // CB
    time_count = WINDOWS // WD
    cell_count = block_count * time_count
    count_key, chosen_key, perm_key = jax.random.split(jax.random.fold_in(key, 11), 3)
    counts = jax.random.randint(count_key, (cell_count,), SEGS_DEV // 8, CAP + 1)
    chosen = jax.random.randint(chosen_key, (), 0, cell_count)
    counts = jnp.where(jnp.arange(cell_count) == chosen, CAP, counts)
    cell_keys = jax.random.split(perm_key, cell_count)
    ranked = jax.vmap(lambda cell_key: jax.random.permutation(cell_key, SEGS_DEV))(cell_keys)
    marks = (ranked < counts[:, None]).astype(jnp.int32)
    marks = marks.reshape(block_count, time_count, CB, WD, S).transpose(0, 2, 1, 3, 4)
    return marks.reshape(C, WINDOWS, S)


def draw_panel_owner(key, part):
    block_count = C // CB
    middle_key, order_key = jax.random.split(jax.random.fold_in(key, 23), 2)
    middle = (jax.random.permutation(middle_key, block_count - 2)[:NP - 2] + 1).astype(jnp.int32)
    joined = jnp.concatenate([jnp.zeros((1,), jnp.int32), middle, jnp.full((1,), block_count - 1, jnp.int32)])
    return jax.random.permutation(order_key, joined).astype(jnp.int32)


def draw_panel_start(key, part):
    start_key, chosen_key = jax.random.split(jax.random.fold_in(key, 37), 2)
    starts = jax.random.randint(start_key, (NP,), 0, CB // PP).astype(jnp.int32)
    chosen = jax.random.randint(chosen_key, (), 0, NP)
    places = jnp.arange(NP, dtype=jnp.int32)
    starts = jnp.where(places == chosen, CB // PP - 1, starts)
    starts = jnp.where(places == (chosen + 1) % NP, 0, starts)
    return (starts * PP).astype(jnp.int32)


def setup_inputs(seed: int = 0) -> dict:
    key_list = jax.random.split(jax.random.key(seed), 5)
    return {
        "traces": draw_traces(jax.random.fold_in(key_list[4], 71), 0),
        "valid": draw_valid(jax.random.fold_in(key_list[4], 71), 0),
        "panel_owner": draw_panel_owner(jax.random.fold_in(key_list[4], 71), 0),
        "panel_start": draw_panel_start(jax.random.fold_in(key_list[4], 71), 0),
    }


def forward_table(length):
    sample = jnp.arange(length, dtype=jnp.int32)
    bin_index = jnp.arange(length // 2, dtype=jnp.int32)
    angles = (sample[:, None] * bin_index[None, :] % length).astype(jnp.float32) * (2.0 * math.pi / length)
    return jnp.concatenate([jnp.cos(angles), -jnp.sin(angles)], axis=1).astype(jnp.bfloat16)

def inverse_table(length, factor):
    bin_index = jnp.arange(length // 2, dtype=jnp.int32)
    lag_index = jnp.arange(length, dtype=jnp.int32)
    angles = (bin_index[:, None] * lag_index[None, :] % length).astype(jnp.float32) * (2.0 * math.pi / length)
    weight = jnp.where(bin_index == 0, 1.0, 2.0).astype(jnp.float32)[:, None] * factor
    return jnp.concatenate([weight * jnp.cos(angles), -weight * jnp.sin(angles)], axis=0)

def whiten(segment_rows, valid_mask, forward):
    spectrum = jnp.dot(segment_rows, forward, preferred_element_type=jnp.float32)
    energy = lax.optimization_barrier(jnp.mean(spectrum * spectrum, axis=1, keepdims=True))
    return (spectrum * lax.rsqrt(energy + 1e-06) * valid_mask[:, None].astype(jnp.float32)).astype(jnp.bfloat16)

def correlate(left, right):
    bins = left.shape[-1] // 2
    left = left.astype(jnp.float32)
    right = right.astype(jnp.float32)
    left_both = jnp.concatenate([left[..., :bins], left[..., bins:]], axis=1)
    right_both = jnp.concatenate([right[..., :bins], right[..., bins:]], axis=1)
    right_turn = jnp.concatenate([right[..., bins:], -right[..., :bins]], axis=1)
    real_part = jnp.einsum('jmk,imk->jik', left_both, right_both)
    imag_part = jnp.einsum('jmk,imk->jik', left_both, right_turn)
    return jnp.concatenate([real_part, imag_part], axis=-1)

def reference(traces, valid, panel_owner, panel_start):
    forward = forward_table(L)
    inverse = inverse_table(L, 1.0 / math.sqrt(F * WINDOWS * S))
    offsets = jnp.arange(PP, dtype=jnp.int32)
    source = (panel_owner[:, None] * CB + panel_start[:, None] + offsets[None, :]).reshape(P_SIZE).astype(jnp.int32)
    panel_rows = traces[source].reshape(P_SIZE * WINDOWS * S, L)
    panel_mask = valid[source].reshape(P_SIZE * WINDOWS * S)
    sources = whiten(panel_rows, panel_mask, forward).reshape(P_SIZE, WINDOWS * S, 2 * F)

    def one_block(block_args):
        block_traces, block_valid = block_args
        whitened = whiten(block_traces.reshape(CB * WINDOWS * S, L), block_valid.reshape(CB * WINDOWS * S), forward)
        cross_spec = correlate(sources, whitened.reshape(CB, WINDOWS * S, 2 * F))
        return jnp.dot(cross_spec, inverse, precision=lax.Precision.HIGHEST)
    blocks = lax.map(one_block, (traces.reshape(C // CB, CB, WINDOWS, S, L), valid.reshape(C // CB, CB, WINDOWS, S)))
    return blocks.transpose(1, 0, 2, 3).reshape(P_SIZE, C, L)
```

```python
import math

import jax
import jax.numpy as jnp
from jax import lax
from jax.sharding import PartitionSpec as P

PP = 4
NP = 4


def spread(value, axis, source):
    kept = jnp.where(lax.axis_index(axis) == source, value, 0).astype(value.dtype)
    return lax.psum(kept, axis)


def forward_table(length):
    sample = jnp.arange(length, dtype=jnp.int32)
    bin_index = jnp.arange(length // 2, dtype=jnp.int32)
    angles = (sample[:, None] * bin_index[None, :] % length).astype(jnp.float32) * (
        2.0 * math.pi / length
    )
    return jnp.concatenate([jnp.cos(angles), -jnp.sin(angles)], axis=1).astype(jnp.bfloat16)


def inverse_table(length, factor):
    bin_index = jnp.arange(length // 2, dtype=jnp.int32)
    lag_index = jnp.arange(length, dtype=jnp.int32)
    angles = (bin_index[:, None] * lag_index[None, :] % length).astype(jnp.float32) * (
        2.0 * math.pi / length
    )
    weight = jnp.where(bin_index == 0, 1.0, 2.0).astype(jnp.float32)[:, None] * factor
    return jnp.concatenate([weight * jnp.cos(angles), -weight * jnp.sin(angles)], axis=0)


def whiten(segment_rows, valid_mask, forward):
    spectrum = jnp.dot(segment_rows, forward, preferred_element_type=jnp.float32)
    energy = jnp.mean(spectrum * spectrum, axis=1, keepdims=True)
    return (spectrum * lax.rsqrt(energy + 1e-06) * valid_mask[:, None].astype(jnp.float32)).astype(
        jnp.bfloat16
    )


def spectra_rows(segment_rows, valid_mask, forward):
    return whiten(segment_rows, valid_mask, forward)


def correlate(left, right):
    bins = left.shape[-1] // 2
    left_both = jnp.concatenate([left[..., :bins], left[..., bins:]], axis=1)
    right_both = jnp.concatenate([right[..., :bins], right[..., bins:]], axis=1)
    right_turn = jnp.concatenate([right[..., bins:], -right[..., :bins]], axis=1)
    real_part = jnp.einsum(
        "jmk,imk->jik", left_both, right_both, preferred_element_type=jnp.float32
    )
    imag_part = jnp.einsum(
        "jmk,imk->jik", left_both, right_turn, preferred_element_type=jnp.float32
    )
    return jnp.concatenate([real_part, imag_part], axis=-1)


def fetch_panel(whitened, panel_root, panel_first):
    candidate = lax.dynamic_slice_in_dim(whitened, panel_first, PP, 0)
    return spread(candidate, "block", panel_root)


def on_device(traces, valid, panel_owner, panel_start):
    channels, windows_here, segments, length = traces.shape
    bins = length // 2
    forward = forward_table(length)
    whitened = spectra_rows(
        traces.reshape(channels * windows_here * segments, length),
        valid.reshape(channels * windows_here * segments),
        forward,
    )
    whitened = whitened.reshape(channels, windows_here, segments, 2 * bins)
    pieces = []
    for panel in range(NP):
        pieces.append(fetch_panel(whitened, panel_owner[panel], panel_start[panel]))
    sources = jnp.concatenate(pieces, axis=0)
    groups = lax.axis_size("tm")
    inverse = inverse_table(length, 1.0 / math.sqrt(bins * windows_here * segments * groups))
    source_count = sources.shape[0]
    own_rows = whitened.reshape(channels, windows_here * segments, 2 * bins)
    source_rows = sources.reshape(source_count, windows_here * segments, 2 * bins)
    stacked = lax.psum_scatter(
        correlate(source_rows, own_rows), "tm", scatter_dimension=0, tiled=True
    )
    return jnp.dot(stacked, inverse, precision=lax.Precision.HIGHEST)


def edge_first(values, groups):
    return lax.ppermute(values, "tm", [(0, 1), (groups - 1, groups - 2)])


def on_line(traces, valid, panel_owner, panel_start):
    channels, windows_here, segments, length = traces.shape
    bins = length // 2
    groups = lax.axis_size("tm")
    place = lax.axis_index("tm")
    forward = forward_table(length)
    whitened = spectra_rows(
        traces.reshape(channels * windows_here * segments, length),
        valid.reshape(channels * windows_here * segments),
        forward,
    ).reshape(channels, windows_here * segments, 2 * bins)
    pieces = []
    for panel in range(NP):
        pieces.append(fetch_panel(whitened, panel_owner[panel], panel_start[panel]))
    sources = jnp.concatenate(pieces, axis=0)
    source_count = sources.shape[0]
    per_group = source_count // groups
    half = source_count // 2
    edge_sources = edge_first(sources, groups)
    inverse = inverse_table(length, 1.0 / math.sqrt(bins * windows_here * segments * groups))
    first_half = place < groups // 2
    chunks = 4
    width = channels // chunks
    outs = []
    for chunk in range(chunks):
        own = whitened[chunk * width:(chunk + 1) * width]
        edge_rows = edge_first(own, groups)
        partial = correlate(sources, own) + correlate(edge_sources, edge_rows)
        low = partial[:half]
        high = partial[half:]
        to_right = lax.ppermute(high, "tm", [(1, 2)])
        to_left = lax.ppermute(low, "tm", [(2, 1)])
        total = jnp.where(first_half, low + to_left, high + to_right)
        lower = total[:per_group]
        upper = total[per_group:]
        back_left = lax.ppermute(lower, "tm", [(1, 0)])
        back_right = lax.ppermute(upper, "tm", [(2, 3)])
        final = jnp.where(
            place == 0,
            back_left,
            jnp.where(place == groups - 1, back_right, jnp.where(first_half, upper, lower)),
        )
        outs.append(jnp.dot(final, inverse, precision=lax.Precision.HIGHEST))
    return jnp.concatenate(outs, axis=1)


def solution(mesh):
    in_specs = (P("block", "tm", None, None), P("block", "tm", None), P(), P())
    out_specs = P("tm", "block", None)
    body = on_line if mesh.shape["tm"] == 4 else on_device
    return jax.shard_map(
        body, mesh=mesh, in_specs=in_specs, out_specs=out_specs, check_vma=False
    )
```

```python
import math

import jax
import jax.numpy as jnp
from jax import lax
from jax.sharding import PartitionSpec as P
from jax.experimental import pallas as pl
from jax.experimental.pallas import tpu as pltpu

PP = 4
NP = 4


def spread(value, axis, source):
    kept = jnp.where(lax.axis_index(axis) == source, value, 0).astype(value.dtype)
    return lax.psum(kept, axis)


def forward_table(length):
    sample = jnp.arange(length, dtype=jnp.int32)
    bin_index = jnp.arange(length // 2, dtype=jnp.int32)
    angles = (sample[:, None] * bin_index[None, :] % length).astype(jnp.float32) * (
        2.0 * math.pi / length
    )
    return jnp.concatenate([jnp.cos(angles), -jnp.sin(angles)], axis=1).astype(jnp.bfloat16)


def inverse_table(length, factor):
    bin_index = jnp.arange(length // 2, dtype=jnp.int32)
    lag_index = jnp.arange(length, dtype=jnp.int32)
    angles = (bin_index[:, None] * lag_index[None, :] % length).astype(jnp.float32) * (
        2.0 * math.pi / length
    )
    weight = jnp.where(bin_index == 0, 1.0, 2.0).astype(jnp.float32)[:, None] * factor
    return jnp.concatenate([weight * jnp.cos(angles), -weight * jnp.sin(angles)], axis=0)


def whiten(segment_rows, valid_mask, forward):
    spectrum = jnp.dot(segment_rows, forward, preferred_element_type=jnp.float32)
    energy = jnp.mean(spectrum * spectrum, axis=1, keepdims=True)
    return (spectrum * lax.rsqrt(energy + 1e-06) * valid_mask[:, None].astype(jnp.float32)).astype(
        jnp.bfloat16
    )


def spectra_rows(segment_rows, valid_mask, forward):
    return whiten(segment_rows, valid_mask, forward)


def correlate(left, right):
    bins = left.shape[-1] // 2
    left_both = jnp.concatenate([left[..., :bins], left[..., bins:]], axis=1)
    right_both = jnp.concatenate([right[..., :bins], right[..., bins:]], axis=1)
    right_turn = jnp.concatenate([right[..., bins:], -right[..., :bins]], axis=1)
    real_part = jnp.einsum(
        "jmk,imk->jik", left_both, right_both, preferred_element_type=jnp.float32
    )
    imag_part = jnp.einsum(
        "jmk,imk->jik", left_both, right_turn, preferred_element_type=jnp.float32
    )
    return jnp.concatenate([real_part, imag_part], axis=-1)


def fetch_panel(whitened, panel_root, panel_first):
    candidate = lax.dynamic_slice_in_dim(whitened, panel_first, PP, 0)
    return spread(candidate, "block", panel_root)


def on_device(traces, valid, panel_owner, panel_start):
    channels, windows_here, segments, length = traces.shape
    bins = length // 2
    forward = forward_table(length)
    whitened = spectra_rows(
        traces.reshape(channels * windows_here * segments, length),
        valid.reshape(channels * windows_here * segments),
        forward,
    )
    whitened = whitened.reshape(channels, windows_here, segments, 2 * bins)
    pieces = []
    for panel in range(NP):
        pieces.append(fetch_panel(whitened, panel_owner[panel], panel_start[panel]))
    sources = jnp.concatenate(pieces, axis=0)
    groups = lax.axis_size("tm")
    inverse = inverse_table(length, 1.0 / math.sqrt(bins * windows_here * segments * groups))
    source_count = sources.shape[0]
    own_rows = whitened.reshape(channels, windows_here * segments, 2 * bins)
    source_rows = sources.reshape(source_count, windows_here * segments, 2 * bins)
    stacked = lax.psum_scatter(
        correlate(source_rows, own_rows), "tm", scatter_dimension=0, tiled=True
    )
    return jnp.dot(stacked, inverse, precision=lax.Precision.HIGHEST)


def edge_first(values, groups):
    return lax.ppermute(values, "tm", [(0, 1), (groups - 1, groups - 2)])


def whiten_kernel(rows_ref, forward_ref, mask_ref, out_ref):
    spectrum = jnp.dot(rows_ref[...], forward_ref[...], preferred_element_type=jnp.float32)
    energy = jnp.mean(spectrum * spectrum, axis=1, keepdims=True)
    scaled = spectrum * lax.rsqrt(energy + 1e-06) * mask_ref[...]
    out_ref[...] = scaled.astype(jnp.bfloat16).reshape(out_ref.shape)


def whiten_segments(rows, mask, forward, chunks):
    segments, channels, length = rows.shape
    width = channels // chunks
    return pl.pallas_call(
        whiten_kernel,
        grid=(segments,),
        in_specs=[
            pl.BlockSpec((None, channels, length), lambda m: (m, 0, 0)),
            pl.BlockSpec((length, length), lambda m: (0, 0)),
            pl.BlockSpec((None, channels, 1), lambda m: (m, 0, 0)),
        ],
        out_specs=pl.BlockSpec((chunks, None, width, length), lambda m: (0, m, 0, 0)),
        out_shape=jax.ShapeDtypeStruct((chunks, segments, width, length), jnp.bfloat16),
    )(rows, forward, mask)


LANES = 128
ROWS = 8


def cross_kernel(own_ref, edge_ref, own_src_ref, edge_src_ref, out_ref):
    segments = own_ref.shape[0]
    sources = own_src_ref.shape[1]
    bins = own_ref.shape[-1] // 2
    for half in range(own_ref.shape[1] // ROWS):
        rows = pl.ds(half * ROWS, ROWS)
        for tile in range(bins // LANES):
            re_lanes = pl.ds(tile * LANES, LANES)
            im_lanes = pl.ds(bins + tile * LANES, LANES)

            def step(m, acc, data_ref, src_ref):
                wr = data_ref[m, rows, re_lanes].astype(jnp.float32)
                wi = data_ref[m, rows, im_lanes].astype(jnp.float32)
                out = []
                for j in range(sources):
                    sr = src_ref[m, j, :, re_lanes]
                    si = src_ref[m, j, :, im_lanes]
                    out.append(acc[2 * j] + (wr * sr + wi * si))
                    out.append(acc[2 * j + 1] + (wi * sr - wr * si))
                return tuple(out)

            acc = tuple(jnp.zeros((ROWS, LANES), jnp.float32) for _ in range(2 * sources))
            acc = lax.fori_loop(0, segments, lambda m, a: step(m, a, own_ref, own_src_ref), acc)
            acc = lax.fori_loop(0, segments, lambda m, a: step(m, a, edge_ref, edge_src_ref), acc)
            for j in range(sources):
                out_ref[j, rows, re_lanes] = acc[2 * j]
                out_ref[j, rows, im_lanes] = acc[2 * j + 1]


def cross_chunk(own, edge, own_src, edge_src):
    segments, width, length = own.shape
    sources = own_src.shape[1]
    step_rows = 2 * ROWS
    return pl.pallas_call(
        cross_kernel,
        grid=(width // step_rows,),
        in_specs=[
            pl.BlockSpec((segments, step_rows, length), lambda i: (0, i, 0)),
            pl.BlockSpec((segments, step_rows, length), lambda i: (0, i, 0)),
            pl.BlockSpec((segments, sources, ROWS, length), lambda i: (0, 0, 0, 0)),
            pl.BlockSpec((segments, sources, ROWS, length), lambda i: (0, 0, 0, 0)),
        ],
        out_specs=pl.BlockSpec((sources, step_rows, length), lambda i: (0, i, 0)),
        out_shape=jax.ShapeDtypeStruct((sources, width, length), jnp.float32),
    )(own, edge, own_src, edge_src)


def on_line(traces, valid, panel_owner, panel_start):
    channels, windows_here, segments, length = traces.shape
    bins = length // 2
    groups = lax.axis_size("tm")
    place = lax.axis_index("tm")
    chunks = 4
    width = channels // chunks
    seg_count = windows_here * segments
    forward = forward_table(length)
    rows = traces.reshape(channels, seg_count, length).transpose(1, 0, 2)
    mask = valid.reshape(channels, seg_count).transpose(1, 0).astype(jnp.float32)[:, :, None]
    whitened = whiten_segments(rows, mask, forward, chunks)
    block_place = lax.axis_index("block")
    pieces = []
    for panel in range(NP):
        first = panel_start[panel]
        chunk_of = first // width
        candidate = lax.dynamic_slice_in_dim(
            lax.dynamic_index_in_dim(whitened, chunk_of, 0, keepdims=False), first - chunk_of * width, PP, 1
        )
        pieces.append(jnp.where(block_place == panel_owner[panel], candidate, 0).astype(candidate.dtype))
    sources = lax.psum(jnp.concatenate(pieces, axis=1), "block")
    source_count = sources.shape[1]
    per_group = source_count // groups
    half = source_count // 2
    edge_sources = edge_first(sources, groups)
    own_wide = jnp.broadcast_to(sources.astype(jnp.float32)[:, :, None, :], (seg_count, source_count, ROWS, length))
    edge_wide = jnp.broadcast_to(edge_sources.astype(jnp.float32)[:, :, None, :], (seg_count, source_count, ROWS, length))
    inverse = inverse_table(length, 1.0 / math.sqrt(bins * seg_count * groups))
    first_half = place < groups // 2
    outs = []
    for chunk in range(chunks):
        own = whitened[chunk]
        edge_rows = edge_first(own, groups)
        partial = cross_chunk(own, edge_rows, own_wide, edge_wide)
        low = partial[:half]
        high = partial[half:]
        to_right = lax.ppermute(high, "tm", [(1, 2)])
        to_left = lax.ppermute(low, "tm", [(2, 1)])
        total = jnp.where(first_half, low + to_left, high + to_right)
        lower = total[:per_group]
        upper = total[per_group:]
        back_left = lax.ppermute(lower, "tm", [(1, 0)])
        back_right = lax.ppermute(upper, "tm", [(2, 3)])
        final = jnp.where(
            place == 0,
            back_left,
            jnp.where(place == groups - 1, back_right, jnp.where(first_half, upper, lower)),
        )
        outs.append(jnp.dot(final, inverse, precision=lax.Precision.HIGHEST))
    return jnp.concatenate(outs, axis=1)


def solution(mesh):
    in_specs = (P("block", "tm", None, None), P("block", "tm", None), P(), P())
    out_specs = P("tm", "block", None)
    body = on_line if mesh.shape["tm"] == 4 else on_device
    return jax.shard_map(
        body, mesh=mesh, in_specs=in_specs, out_specs=out_specs, check_vma=False
    )
```

```python
import math

import jax
import jax.numpy as jnp
from jax import lax
from jax.sharding import PartitionSpec as P
from jax.experimental import pallas as pl
from jax.experimental.pallas import tpu as pltpu

PP = 4
NP = 4


def spread(value, axis, source):
    kept = jnp.where(lax.axis_index(axis) == source, value, 0).astype(value.dtype)
    return lax.psum(kept, axis)


def forward_table(length):
    sample = jnp.arange(length, dtype=jnp.int32)
    bin_index = jnp.arange(length // 2, dtype=jnp.int32)
    angles = (sample[:, None] * bin_index[None, :] % length).astype(jnp.float32) * (
        2.0 * math.pi / length
    )
    return jnp.concatenate([jnp.cos(angles), -jnp.sin(angles)], axis=1).astype(jnp.bfloat16)


def inverse_table(length, factor):
    bin_index = jnp.arange(length // 2, dtype=jnp.int32)
    lag_index = jnp.arange(length, dtype=jnp.int32)
    angles = (bin_index[:, None] * lag_index[None, :] % length).astype(jnp.float32) * (
        2.0 * math.pi / length
    )
    weight = jnp.where(bin_index == 0, 1.0, 2.0).astype(jnp.float32)[:, None] * factor
    return jnp.concatenate([weight * jnp.cos(angles), -weight * jnp.sin(angles)], axis=0)


def whiten(segment_rows, valid_mask, forward):
    spectrum = jnp.dot(segment_rows, forward, preferred_element_type=jnp.float32)
    energy = jnp.mean(spectrum * spectrum, axis=1, keepdims=True)
    return (spectrum * lax.rsqrt(energy + 1e-06) * valid_mask[:, None].astype(jnp.float32)).astype(
        jnp.bfloat16
    )


def spectra_rows(segment_rows, valid_mask, forward):
    return whiten(segment_rows, valid_mask, forward)


def correlate(left, right):
    bins = left.shape[-1] // 2
    left_both = jnp.concatenate([left[..., :bins], left[..., bins:]], axis=1)
    right_both = jnp.concatenate([right[..., :bins], right[..., bins:]], axis=1)
    right_turn = jnp.concatenate([right[..., bins:], -right[..., :bins]], axis=1)
    real_part = jnp.einsum(
        "jmk,imk->jik", left_both, right_both, preferred_element_type=jnp.float32
    )
    imag_part = jnp.einsum(
        "jmk,imk->jik", left_both, right_turn, preferred_element_type=jnp.float32
    )
    return jnp.concatenate([real_part, imag_part], axis=-1)


def fetch_panel(whitened, panel_root, panel_first):
    candidate = lax.dynamic_slice_in_dim(whitened, panel_first, PP, 0)
    return spread(candidate, "block", panel_root)


def on_device(traces, valid, panel_owner, panel_start):
    channels, windows_here, segments, length = traces.shape
    bins = length // 2
    forward = forward_table(length)
    whitened = spectra_rows(
        traces.reshape(channels * windows_here * segments, length),
        valid.reshape(channels * windows_here * segments),
        forward,
    )
    whitened = whitened.reshape(channels, windows_here, segments, 2 * bins)
    pieces = []
    for panel in range(NP):
        pieces.append(fetch_panel(whitened, panel_owner[panel], panel_start[panel]))
    sources = jnp.concatenate(pieces, axis=0)
    groups = lax.axis_size("tm")
    inverse = inverse_table(length, 1.0 / math.sqrt(bins * windows_here * segments * groups))
    source_count = sources.shape[0]
    own_rows = whitened.reshape(channels, windows_here * segments, 2 * bins)
    source_rows = sources.reshape(source_count, windows_here * segments, 2 * bins)
    stacked = lax.psum_scatter(
        correlate(source_rows, own_rows), "tm", scatter_dimension=0, tiled=True
    )
    return jnp.dot(stacked, inverse, precision=lax.Precision.HIGHEST)


def edge_first(values, groups):
    return lax.ppermute(values, "tm", [(0, 1), (groups - 1, groups - 2)])


def whiten_kernel(rows_ref, forward_ref, mask_ref, out_ref):
    spectrum = jnp.dot(rows_ref[...], forward_ref[...], preferred_element_type=jnp.float32)
    energy = jnp.mean(spectrum * spectrum, axis=1, keepdims=True)
    scaled = spectrum * lax.rsqrt(energy + 1e-06) * mask_ref[...]
    out_ref[...] = scaled.astype(jnp.bfloat16).reshape(out_ref.shape)


def whiten_segments(rows, mask, forward, chunks):
    segments, channels, length = rows.shape
    width = channels // chunks
    return pl.pallas_call(
        whiten_kernel,
        grid=(segments,),
        in_specs=[
            pl.BlockSpec((None, channels, length), lambda m: (m, 0, 0)),
            pl.BlockSpec((length, length), lambda m: (0, 0)),
            pl.BlockSpec((None, channels, 1), lambda m: (m, 0, 0)),
        ],
        out_specs=pl.BlockSpec((chunks, None, width, length), lambda m: (0, m, 0, 0)),
        out_shape=jax.ShapeDtypeStruct((chunks, segments, width, length), jnp.bfloat16),
    )(rows, forward, mask)


LANES = 128
ROWS = 8


def cross_kernel(own_ref, edge_ref, own_src_ref, edge_src_ref, out_ref):
    segments = own_ref.shape[0]
    sources = own_src_ref.shape[1]
    bins = own_ref.shape[-1] // 2
    for half in range(own_ref.shape[1] // ROWS):
        rows = pl.ds(half * ROWS, ROWS)
        for tile in range(bins // LANES):
            re_lanes = pl.ds(tile * LANES, LANES)
            im_lanes = pl.ds(bins + tile * LANES, LANES)

            def step(m, acc, data_ref, src_ref):
                wr = data_ref[m, rows, re_lanes].astype(jnp.float32)
                wi = data_ref[m, rows, im_lanes].astype(jnp.float32)
                out = []
                for j in range(sources):
                    sr = src_ref[m, j, :, re_lanes]
                    si = src_ref[m, j, :, im_lanes]
                    out.append(acc[2 * j] + (wr * sr + wi * si))
                    out.append(acc[2 * j + 1] + (wi * sr - wr * si))
                return tuple(out)

            acc = tuple(jnp.zeros((ROWS, LANES), jnp.float32) for _ in range(2 * sources))
            acc = lax.fori_loop(0, segments, lambda m, a: step(m, a, own_ref, own_src_ref), acc)
            acc = lax.fori_loop(0, segments, lambda m, a: step(m, a, edge_ref, edge_src_ref), acc)
            for j in range(sources):
                out_ref[j, rows, re_lanes] = acc[2 * j]
                out_ref[j, rows, im_lanes] = acc[2 * j + 1]


def cross_chunk(own, edge, own_src, edge_src):
    segments, width, length = own.shape
    sources = own_src.shape[1]
    step_rows = 2 * ROWS
    return pl.pallas_call(
        cross_kernel,
        grid=(width // step_rows,),
        in_specs=[
            pl.BlockSpec((segments, step_rows, length), lambda i: (0, i, 0)),
            pl.BlockSpec((segments, step_rows, length), lambda i: (0, i, 0)),
            pl.BlockSpec((segments, sources, ROWS, length), lambda i: (0, 0, 0, 0)),
            pl.BlockSpec((segments, sources, ROWS, length), lambda i: (0, 0, 0, 0)),
        ],
        out_specs=pl.BlockSpec((sources, step_rows, length), lambda i: (0, i, 0)),
        out_shape=jax.ShapeDtypeStruct((sources, width, length), jnp.float32),
    )(own, edge, own_src, edge_src)


def butterfly_sum(values, axis):
    count = lax.axis_size(axis)
    step = 1
    while step < count:
        values = values + lax.ppermute(values, axis, [(b, b ^ step) for b in range(count)])
        step *= 2
    return values


def widen(values, length):
    segments, count = values.shape[0], values.shape[1]
    return jnp.broadcast_to(values.astype(jnp.float32)[:, :, None, :], (segments, count, ROWS, length))


def on_line(traces, valid, panel_owner, panel_start):
    channels, windows_here, segments, length = traces.shape
    bins = length // 2
    groups = lax.axis_size("tm")
    place = lax.axis_index("tm")
    chunks = 8
    width = channels // chunks
    seg_count = windows_here * segments
    forward = forward_table(length)
    rows = traces.reshape(channels, seg_count, length).transpose(1, 0, 2)
    mask = valid.reshape(channels, seg_count).transpose(1, 0).astype(jnp.float32)[:, :, None]
    whitened = whiten_segments(rows, mask, forward, chunks)
    block_place = lax.axis_index("block")
    pieces = []
    for panel in range(NP):
        first = panel_start[panel]
        chunk_of = first // width
        candidate = lax.dynamic_slice_in_dim(
            lax.dynamic_index_in_dim(whitened, chunk_of, 0, keepdims=False), first - chunk_of * width, PP, 1
        )
        pieces.append(jnp.where(block_place == panel_owner[panel], candidate, 0).astype(candidate.dtype))
    sources = butterfly_sum(jnp.concatenate(pieces, axis=1), "block")
    source_count = sources.shape[1]
    per_group = source_count // groups
    half = source_count // 2
    first_half = place < groups // 2
    turned = jnp.concatenate(
        [sources[:, source_count - per_group:], sources[:, half:source_count - per_group]], axis=1
    )
    far = jnp.where(first_half, turned, sources[:, :half])
    near = jnp.where(first_half, sources[:, :half], turned)
    edge_far = edge_first(far, groups)
    edge_near = edge_first(near, groups)
    far_wide, edge_far_wide = widen(far, length), widen(edge_far, length)
    near_wide, edge_near_wide = widen(near, length), widen(edge_near, length)
    inverse = inverse_table(length, 1.0 / math.sqrt(bins * seg_count * groups))
    is_edge = jnp.logical_or(place == 0, place == groups - 1)
    outs = []
    for chunk in range(chunks):
        own = whitened[chunk]
        edge_rows = edge_first(own, groups)
        far_part = cross_chunk(own, edge_rows, far_wide, edge_far_wide)
        got = lax.ppermute(far_part, "tm", [(1, 2), (2, 1)])
        total = cross_chunk(own, edge_rows, near_wide, edge_near_wide) + got
        back = lax.ppermute(total[:per_group], "tm", [(1, 0), (2, 3)])
        final = jnp.where(is_edge, back, total[per_group:])
        outs.append(jnp.dot(final, inverse, precision=lax.Precision.HIGHEST))
    return jnp.concatenate(outs, axis=1)


def solution(mesh):
    in_specs = (P("block", "tm", None, None), P("block", "tm", None), P(), P())
    out_specs = P("tm", "block", None)
    body = on_line if mesh.shape["tm"] == 4 else on_device
    return jax.shard_map(
        body, mesh=mesh, in_specs=in_specs, out_specs=out_specs, check_vma=False
    )
```

```python
import math

import jax
import jax.numpy as jnp
from jax import lax
from jax.sharding import PartitionSpec as P
from jax.experimental import pallas as pl
from jax.experimental.pallas import tpu as pltpu

PP = 4
NP = 4


def spread(value, axis, source):
    kept = jnp.where(lax.axis_index(axis) == source, value, 0).astype(value.dtype)
    return lax.psum(kept, axis)


def forward_table(length):
    sample = jnp.arange(length, dtype=jnp.int32)
    bin_index = jnp.arange(length // 2, dtype=jnp.int32)
    angles = (sample[:, None] * bin_index[None, :] % length).astype(jnp.float32) * (
        2.0 * math.pi / length
    )
    return jnp.concatenate([jnp.cos(angles), -jnp.sin(angles)], axis=1).astype(jnp.bfloat16)


def inverse_table(length, factor):
    bin_index = jnp.arange(length // 2, dtype=jnp.int32)
    lag_index = jnp.arange(length, dtype=jnp.int32)
    angles = (bin_index[:, None] * lag_index[None, :] % length).astype(jnp.float32) * (
        2.0 * math.pi / length
    )
    weight = jnp.where(bin_index == 0, 1.0, 2.0).astype(jnp.float32)[:, None] * factor
    return jnp.concatenate([weight * jnp.cos(angles), -weight * jnp.sin(angles)], axis=0)


def whiten(segment_rows, valid_mask, forward):
    spectrum = jnp.dot(segment_rows, forward, preferred_element_type=jnp.float32)
    energy = jnp.mean(spectrum * spectrum, axis=1, keepdims=True)
    return (spectrum * lax.rsqrt(energy + 1e-06) * valid_mask[:, None].astype(jnp.float32)).astype(
        jnp.bfloat16
    )


def spectra_rows(segment_rows, valid_mask, forward):
    return whiten(segment_rows, valid_mask, forward)


def correlate(left, right):
    bins = left.shape[-1] // 2
    left_both = jnp.concatenate([left[..., :bins], left[..., bins:]], axis=1)
    right_both = jnp.concatenate([right[..., :bins], right[..., bins:]], axis=1)
    right_turn = jnp.concatenate([right[..., bins:], -right[..., :bins]], axis=1)
    real_part = jnp.einsum(
        "jmk,imk->jik", left_both, right_both, preferred_element_type=jnp.float32
    )
    imag_part = jnp.einsum(
        "jmk,imk->jik", left_both, right_turn, preferred_element_type=jnp.float32
    )
    return jnp.concatenate([real_part, imag_part], axis=-1)


def fetch_panel(whitened, panel_root, panel_first):
    candidate = lax.dynamic_slice_in_dim(whitened, panel_first, PP, 0)
    return spread(candidate, "block", panel_root)


def on_device(traces, valid, panel_owner, panel_start):
    channels, windows_here, segments, length = traces.shape
    bins = length // 2
    forward = forward_table(length)
    whitened = spectra_rows(
        traces.reshape(channels * windows_here * segments, length),
        valid.reshape(channels * windows_here * segments),
        forward,
    )
    whitened = whitened.reshape(channels, windows_here, segments, 2 * bins)
    pieces = []
    for panel in range(NP):
        pieces.append(fetch_panel(whitened, panel_owner[panel], panel_start[panel]))
    sources = jnp.concatenate(pieces, axis=0)
    groups = lax.axis_size("tm")
    inverse = inverse_table(length, 1.0 / math.sqrt(bins * windows_here * segments * groups))
    source_count = sources.shape[0]
    own_rows = whitened.reshape(channels, windows_here * segments, 2 * bins)
    source_rows = sources.reshape(source_count, windows_here * segments, 2 * bins)
    stacked = lax.psum_scatter(
        correlate(source_rows, own_rows), "tm", scatter_dimension=0, tiled=True
    )
    return jnp.dot(stacked, inverse, precision=lax.Precision.HIGHEST)


def edge_first(values, groups):
    return lax.ppermute(values, "tm", [(0, 1), (groups - 1, groups - 2)])


def whiten_kernel(rows_ref, forward_ref, mask_ref, out_ref):
    spectrum = jnp.dot(rows_ref[...], forward_ref[...], preferred_element_type=jnp.float32)
    energy = jnp.mean(spectrum * spectrum, axis=1, keepdims=True)
    scaled = spectrum * lax.rsqrt(energy + 1e-06) * mask_ref[...]
    out_ref[...] = scaled.astype(jnp.bfloat16).reshape(out_ref.shape)


def whiten_segments(rows, mask, forward, chunks):
    segments, channels, length = rows.shape
    width = channels // chunks
    return pl.pallas_call(
        whiten_kernel,
        grid=(segments,),
        in_specs=[
            pl.BlockSpec((None, channels, length), lambda m: (m, 0, 0)),
            pl.BlockSpec((length, length), lambda m: (0, 0)),
            pl.BlockSpec((None, channels, 1), lambda m: (m, 0, 0)),
        ],
        out_specs=pl.BlockSpec((chunks, None, width, length), lambda m: (0, m, 0, 0)),
        out_shape=jax.ShapeDtypeStruct((chunks, segments, width, length), jnp.bfloat16),
    )(rows, forward, mask)


LANES = 128
ROWS = 8


def cross_kernel(own_ref, edge_ref, own_src_ref, edge_src_ref, out_ref):
    segments = own_ref.shape[0]
    sources = own_src_ref.shape[1]
    bins = own_ref.shape[-1] // 2
    for half in range(own_ref.shape[1] // ROWS):
        rows = pl.ds(half * ROWS, ROWS)
        for tile in range(bins // LANES):
            re_lanes = pl.ds(tile * LANES, LANES)
            im_lanes = pl.ds(bins + tile * LANES, LANES)

            def step(m, acc, data_ref, src_ref):
                wr = data_ref[m, rows, re_lanes].astype(jnp.float32)
                wi = data_ref[m, rows, im_lanes].astype(jnp.float32)
                out = []
                for j in range(sources):
                    sr = src_ref[m, j, :, re_lanes]
                    si = src_ref[m, j, :, im_lanes]
                    out.append(acc[2 * j] + (wr * sr + wi * si))
                    out.append(acc[2 * j + 1] + (wi * sr - wr * si))
                return tuple(out)

            acc = tuple(jnp.zeros((ROWS, LANES), jnp.float32) for _ in range(2 * sources))
            acc = lax.fori_loop(0, segments, lambda m, a: step(m, a, own_ref, own_src_ref), acc)
            acc = lax.fori_loop(0, segments, lambda m, a: step(m, a, edge_ref, edge_src_ref), acc)
            for j in range(sources):
                out_ref[j, rows, re_lanes] = acc[2 * j]
                out_ref[j, rows, im_lanes] = acc[2 * j + 1]


def cross_chunk(own, edge, own_src, edge_src):
    segments, width, length = own.shape
    sources = own_src.shape[1]
    step_rows = 2 * ROWS
    return pl.pallas_call(
        cross_kernel,
        grid=(width // step_rows,),
        in_specs=[
            pl.BlockSpec((segments, step_rows, length), lambda i: (0, i, 0)),
            pl.BlockSpec((segments, step_rows, length), lambda i: (0, i, 0)),
            pl.BlockSpec((segments, sources, ROWS, length), lambda i: (0, 0, 0, 0)),
            pl.BlockSpec((segments, sources, ROWS, length), lambda i: (0, 0, 0, 0)),
        ],
        out_specs=pl.BlockSpec((sources, step_rows, length), lambda i: (0, i, 0)),
        out_shape=jax.ShapeDtypeStruct((sources, width, length), jnp.float32),
    )(own, edge, own_src, edge_src)


def butterfly_sum(values, axis):
    count = lax.axis_size(axis)
    step = 1
    while step < count:
        values = values + lax.ppermute(values, axis, [(b, b ^ step) for b in range(count)])
        step *= 2
    return values


def widen(values, length):
    segments, count = values.shape[0], values.shape[1]
    return jnp.broadcast_to(values.astype(jnp.float32)[:, :, None, :], (segments, count, ROWS, length))


def on_line(traces, valid, panel_owner, panel_start):
    channels, windows_here, segments, length = traces.shape
    bins = length // 2
    groups = lax.axis_size("tm")
    place = lax.axis_index("tm")
    chunks = 8
    width = channels // chunks
    seg_count = windows_here * segments
    forward = forward_table(length)
    rows = traces.reshape(channels, seg_count, length).transpose(1, 0, 2)
    mask = valid.reshape(channels, seg_count).transpose(1, 0).astype(jnp.float32)[:, :, None]
    whitened = whiten_segments(rows, mask, forward, chunks)
    block_place = lax.axis_index("block")
    pieces = []
    for panel in range(NP):
        first = panel_start[panel]
        chunk_of = first // width
        candidate = lax.dynamic_slice_in_dim(
            lax.dynamic_index_in_dim(whitened, chunk_of, 0, keepdims=False), first - chunk_of * width, PP, 1
        )
        pieces.append(jnp.where(block_place == panel_owner[panel], candidate, 0).astype(candidate.dtype))
    sources = butterfly_sum(jnp.concatenate(pieces, axis=1), "block")
    source_count = sources.shape[1]
    per_group = source_count // groups
    half = source_count // 2
    first_half = place < groups // 2
    turned = jnp.concatenate(
        [sources[:, source_count - per_group:], sources[:, half:source_count - per_group]], axis=1
    )
    far = jnp.where(first_half, turned, sources[:, :half])
    near = jnp.where(first_half, sources[:, :half], turned)
    inverse = inverse_table(length, 1.0 / math.sqrt(bins * seg_count * groups))
    is_edge = jnp.logical_or(place == 0, place == groups - 1)
    edge_chunks = [edge_first(whitened[0], groups)]
    pair = jnp.concatenate([far, near], axis=1)
    pair, _ = lax.optimization_barrier((pair, edge_chunks[0]))
    edge_pair = edge_first(pair, groups)
    far_wide, edge_far_wide = widen(far, length), widen(edge_pair[:, :half], length)
    near_wide, edge_near_wide = widen(near, length), widen(edge_pair[:, half:], length)
    previous = edge_pair
    for chunk in range(1, chunks):
        own, _ = lax.optimization_barrier((whitened[chunk], previous))
        previous = edge_first(own, groups)
        edge_chunks.append(previous)
    outs = []
    last_sent = None
    for chunk in range(chunks):
        own = whitened[chunk]
        edge_rows = edge_chunks[chunk]
        far_part = cross_chunk(own, edge_rows, far_wide, edge_far_wide)
        if last_sent is not None:
            far_part, _ = lax.optimization_barrier((far_part, last_sent))
        got = lax.ppermute(far_part, "tm", [(1, 2), (2, 1)])
        last_sent = got
        total = cross_chunk(own, edge_rows, near_wide, edge_near_wide) + got
        back = lax.ppermute(total[:per_group], "tm", [(1, 0), (2, 3)])
        final = jnp.where(is_edge, back, total[per_group:])
        outs.append(jnp.dot(final, inverse, precision=lax.Precision.HIGHEST))
    return jnp.concatenate(outs, axis=1)


def solution(mesh):
    in_specs = (P("block", "tm", None, None), P("block", "tm", None), P(), P())
    out_specs = P("tm", "block", None)
    body = on_line if mesh.shape["tm"] == 4 else on_device
    return jax.shard_map(
        body, mesh=mesh, in_specs=in_specs, out_specs=out_specs, check_vma=False
    )
```

```python
import math

import jax
import jax.numpy as jnp
from jax import lax
from jax.sharding import PartitionSpec as P
from jax.experimental import pallas as pl
from jax.experimental.pallas import tpu as pltpu

PP = 4
NP = 4


def spread(value, axis, source):
    kept = jnp.where(lax.axis_index(axis) == source, value, 0).astype(value.dtype)
    return lax.psum(kept, axis)


def forward_table(length):
    sample = jnp.arange(length, dtype=jnp.int32)
    bin_index = jnp.arange(length // 2, dtype=jnp.int32)
    angles = (sample[:, None] * bin_index[None, :] % length).astype(jnp.float32) * (
        2.0 * math.pi / length
    )
    return jnp.concatenate([jnp.cos(angles), -jnp.sin(angles)], axis=1).astype(jnp.bfloat16)


def inverse_table(length, factor):
    bin_index = jnp.arange(length // 2, dtype=jnp.int32)
    lag_index = jnp.arange(length, dtype=jnp.int32)
    angles = (bin_index[:, None] * lag_index[None, :] % length).astype(jnp.float32) * (
        2.0 * math.pi / length
    )
    weight = jnp.where(bin_index == 0, 1.0, 2.0).astype(jnp.float32)[:, None] * factor
    return jnp.concatenate([weight * jnp.cos(angles), -weight * jnp.sin(angles)], axis=0)


def whiten(segment_rows, valid_mask, forward):
    spectrum = jnp.dot(segment_rows, forward, preferred_element_type=jnp.float32)
    energy = jnp.mean(spectrum * spectrum, axis=1, keepdims=True)
    return (spectrum * lax.rsqrt(energy + 1e-06) * valid_mask[:, None].astype(jnp.float32)).astype(
        jnp.bfloat16
    )


def spectra_rows(segment_rows, valid_mask, forward):
    return whiten(segment_rows, valid_mask, forward)


def correlate(left, right):
    bins = left.shape[-1] // 2
    left_both = jnp.concatenate([left[..., :bins], left[..., bins:]], axis=1)
    right_both = jnp.concatenate([right[..., :bins], right[..., bins:]], axis=1)
    right_turn = jnp.concatenate([right[..., bins:], -right[..., :bins]], axis=1)
    real_part = jnp.einsum(
        "jmk,imk->jik", left_both, right_both, preferred_element_type=jnp.float32
    )
    imag_part = jnp.einsum(
        "jmk,imk->jik", left_both, right_turn, preferred_element_type=jnp.float32
    )
    return jnp.concatenate([real_part, imag_part], axis=-1)


def fetch_panel(whitened, panel_root, panel_first):
    candidate = lax.dynamic_slice_in_dim(whitened, panel_first, PP, 0)
    return spread(candidate, "block", panel_root)


def on_device(traces, valid, panel_owner, panel_start):
    channels, windows_here, segments, length = traces.shape
    bins = length // 2
    forward = forward_table(length)
    whitened = spectra_rows(
        traces.reshape(channels * windows_here * segments, length),
        valid.reshape(channels * windows_here * segments),
        forward,
    )
    whitened = whitened.reshape(channels, windows_here, segments, 2 * bins)
    pieces = []
    for panel in range(NP):
        pieces.append(fetch_panel(whitened, panel_owner[panel], panel_start[panel]))
    sources = jnp.concatenate(pieces, axis=0)
    groups = lax.axis_size("tm")
    inverse = inverse_table(length, 1.0 / math.sqrt(bins * windows_here * segments * groups))
    source_count = sources.shape[0]
    own_rows = whitened.reshape(channels, windows_here * segments, 2 * bins)
    source_rows = sources.reshape(source_count, windows_here * segments, 2 * bins)
    stacked = lax.psum_scatter(
        correlate(source_rows, own_rows), "tm", scatter_dimension=0, tiled=True
    )
    return jnp.dot(stacked, inverse, precision=lax.Precision.HIGHEST)


def edge_first(values, groups):
    return lax.ppermute(values, "tm", [(0, 1), (groups - 1, groups - 2)])


def whiten_kernel(rows_ref, forward_ref, mask_ref, out_ref):
    spectrum = jnp.dot(rows_ref[...], forward_ref[...], preferred_element_type=jnp.float32)
    energy = jnp.mean(spectrum * spectrum, axis=1, keepdims=True)
    scaled = spectrum * lax.rsqrt(energy + 1e-06) * mask_ref[...]
    out_ref[...] = scaled.astype(jnp.bfloat16).reshape(out_ref.shape)


def whiten_segments(rows, mask, forward, chunks):
    segments, channels, length = rows.shape
    width = channels // chunks
    return pl.pallas_call(
        whiten_kernel,
        grid=(segments,),
        in_specs=[
            pl.BlockSpec((None, channels, length), lambda m: (m, 0, 0)),
            pl.BlockSpec((length, length), lambda m: (0, 0)),
            pl.BlockSpec((None, channels, 1), lambda m: (m, 0, 0)),
        ],
        out_specs=pl.BlockSpec((chunks, None, width, length), lambda m: (0, m, 0, 0)),
        out_shape=jax.ShapeDtypeStruct((chunks, segments, width, length), jnp.bfloat16),
    )(rows, forward, mask)


LANES = 128
ROWS = 8


def cross_kernel(own_ref, edge_ref, own_src_ref, edge_src_ref, out_ref):
    segments = own_ref.shape[0]
    sources = own_src_ref.shape[1]
    rows = own_ref.shape[1]
    bins = own_ref.shape[-1] // 2

    def tile_body(tile, carry):
        re_lanes = pl.ds(pl.multiple_of(tile * LANES, LANES), LANES)
        im_lanes = pl.ds(pl.multiple_of(bins + tile * LANES, LANES), LANES)

        def step(m, acc, data_ref, src_ref):
            wr = data_ref[m, :, re_lanes].astype(jnp.float32)
            wi = data_ref[m, :, im_lanes].astype(jnp.float32)
            out = []
            for j in range(sources):
                sr = jnp.concatenate([src_ref[m, j, :, re_lanes]] * (rows // ROWS), axis=0)
                si = jnp.concatenate([src_ref[m, j, :, im_lanes]] * (rows // ROWS), axis=0)
                out.append(acc[2 * j] + (wr * sr + wi * si))
                out.append(acc[2 * j + 1] + (wi * sr - wr * si))
            return tuple(out)

        acc = tuple(jnp.zeros((rows, LANES), jnp.float32) for _ in range(2 * sources))
        acc = lax.fori_loop(0, segments, lambda m, a: step(m, a, own_ref, own_src_ref), acc)
        acc = lax.fori_loop(0, segments, lambda m, a: step(m, a, edge_ref, edge_src_ref), acc)
        for j in range(sources):
            out_ref[j, :, re_lanes] = acc[2 * j]
            out_ref[j, :, im_lanes] = acc[2 * j + 1]
        return carry

    lax.fori_loop(0, bins // LANES, tile_body, 0)


def cross_chunk(own, edge, own_src, edge_src):
    segments, width, length = own.shape
    sources = own_src.shape[1]
    step_rows = 2 * ROWS
    return pl.pallas_call(
        cross_kernel,
        grid=(width // step_rows,),
        in_specs=[
            pl.BlockSpec((segments, step_rows, length), lambda i: (0, i, 0)),
            pl.BlockSpec((segments, step_rows, length), lambda i: (0, i, 0)),
            pl.BlockSpec((segments, sources, ROWS, length), lambda i: (0, 0, 0, 0)),
            pl.BlockSpec((segments, sources, ROWS, length), lambda i: (0, 0, 0, 0)),
        ],
        out_specs=pl.BlockSpec((sources, step_rows, length), lambda i: (0, i, 0)),
        out_shape=jax.ShapeDtypeStruct((sources, width, length), jnp.float32),
    )(own, edge, own_src, edge_src)


def butterfly_sum(values, axis):
    count = lax.axis_size(axis)
    step = 1
    while step < count:
        values = values + lax.ppermute(values, axis, [(b, b ^ step) for b in range(count)])
        step *= 2
    return values


def widen(values, length):
    segments, count = values.shape[0], values.shape[1]
    return jnp.broadcast_to(values.astype(jnp.float32)[:, :, None, :], (segments, count, ROWS, length))


def on_line(traces, valid, panel_owner, panel_start):
    channels, windows_here, segments, length = traces.shape
    bins = length // 2
    groups = lax.axis_size("tm")
    place = lax.axis_index("tm")
    chunks = 8
    width = channels // chunks
    seg_count = windows_here * segments
    forward = forward_table(length)
    rows = traces.reshape(channels, seg_count, length).transpose(1, 0, 2)
    mask = valid.reshape(channels, seg_count).transpose(1, 0).astype(jnp.float32)[:, :, None]
    whitened = whiten_segments(rows, mask, forward, chunks)
    block_place = lax.axis_index("block")
    pieces = []
    for panel in range(NP):
        first = panel_start[panel]
        chunk_of = first // width
        candidate = lax.dynamic_slice_in_dim(
            lax.dynamic_index_in_dim(whitened, chunk_of, 0, keepdims=False), first - chunk_of * width, PP, 1
        )
        pieces.append(jnp.where(block_place == panel_owner[panel], candidate, 0).astype(candidate.dtype))
    sources = butterfly_sum(jnp.concatenate(pieces, axis=1), "block")
    source_count = sources.shape[1]
    per_group = source_count // groups
    half = source_count // 2
    first_half = place < groups // 2
    turned = jnp.concatenate(
        [sources[:, source_count - per_group:], sources[:, half:source_count - per_group]], axis=1
    )
    far = jnp.where(first_half, turned, sources[:, :half])
    near = jnp.where(first_half, sources[:, :half], turned)
    inverse = inverse_table(length, 1.0 / math.sqrt(bins * seg_count * groups))
    is_edge = jnp.logical_or(place == 0, place == groups - 1)
    edge_chunks = [edge_first(whitened[0], groups)]
    pair = jnp.concatenate([far, near], axis=1)
    pair, _ = lax.optimization_barrier((pair, edge_chunks[0]))
    edge_pair = edge_first(pair, groups)
    far_wide, edge_far_wide = widen(far, length), widen(edge_pair[:, :half], length)
    near_wide, edge_near_wide = widen(near, length), widen(edge_pair[:, half:], length)
    previous = edge_pair
    for chunk in range(1, chunks):
        own, _ = lax.optimization_barrier((whitened[chunk], previous))
        previous = edge_first(own, groups)
        edge_chunks.append(previous)
    outs = []
    last_sent = None
    for chunk in range(chunks):
        own = whitened[chunk]
        edge_rows = edge_chunks[chunk]
        far_part = cross_chunk(own, edge_rows, far_wide, edge_far_wide)
        if last_sent is not None:
            far_part, _ = lax.optimization_barrier((far_part, last_sent))
        got = lax.ppermute(far_part, "tm", [(1, 2), (2, 1)])
        last_sent = got
        total = cross_chunk(own, edge_rows, near_wide, edge_near_wide) + got
        back = lax.ppermute(total[:per_group], "tm", [(1, 0), (2, 3)])
        final = jnp.where(is_edge, back, total[per_group:])
        outs.append(jnp.dot(final, inverse, precision=lax.Precision.HIGHEST))
    return jnp.concatenate(outs, axis=1)


def solution(mesh):
    in_specs = (P("block", "tm", None, None), P("block", "tm", None), P(), P())
    out_specs = P("tm", "block", None)
    body = on_line if mesh.shape["tm"] == 4 else on_device
    return jax.shard_map(
        body, mesh=mesh, in_specs=in_specs, out_specs=out_specs, check_vma=False
    )
```

```python
import math

import jax
import jax.numpy as jnp
from jax import lax
from jax.sharding import PartitionSpec as P
from jax.experimental import pallas as pl
from jax.experimental.pallas import tpu as pltpu

PP = 4
NP = 4


def spread(value, axis, source):
    kept = jnp.where(lax.axis_index(axis) == source, value, 0).astype(value.dtype)
    return lax.psum(kept, axis)


def forward_table(length):
    sample = jnp.arange(length, dtype=jnp.int32)
    bin_index = jnp.arange(length // 2, dtype=jnp.int32)
    angles = (sample[:, None] * bin_index[None, :] % length).astype(jnp.float32) * (
        2.0 * math.pi / length
    )
    return jnp.concatenate([jnp.cos(angles), -jnp.sin(angles)], axis=1).astype(jnp.bfloat16)


def inverse_table(length, factor):
    bin_index = jnp.arange(length // 2, dtype=jnp.int32)
    lag_index = jnp.arange(length, dtype=jnp.int32)
    angles = (bin_index[:, None] * lag_index[None, :] % length).astype(jnp.float32) * (
        2.0 * math.pi / length
    )
    weight = jnp.where(bin_index == 0, 1.0, 2.0).astype(jnp.float32)[:, None] * factor
    return jnp.concatenate([weight * jnp.cos(angles), -weight * jnp.sin(angles)], axis=0)


def whiten(segment_rows, valid_mask, forward):
    spectrum = jnp.dot(segment_rows, forward, preferred_element_type=jnp.float32)
    energy = jnp.mean(spectrum * spectrum, axis=1, keepdims=True)
    return (spectrum * lax.rsqrt(energy + 1e-06) * valid_mask[:, None].astype(jnp.float32)).astype(
        jnp.bfloat16
    )


def spectra_rows(segment_rows, valid_mask, forward):
    return whiten(segment_rows, valid_mask, forward)


def correlate(left, right):
    bins = left.shape[-1] // 2
    left_both = jnp.concatenate([left[..., :bins], left[..., bins:]], axis=1)
    right_both = jnp.concatenate([right[..., :bins], right[..., bins:]], axis=1)
    right_turn = jnp.concatenate([right[..., bins:], -right[..., :bins]], axis=1)
    real_part = jnp.einsum(
        "jmk,imk->jik", left_both, right_both, preferred_element_type=jnp.float32
    )
    imag_part = jnp.einsum(
        "jmk,imk->jik", left_both, right_turn, preferred_element_type=jnp.float32
    )
    return jnp.concatenate([real_part, imag_part], axis=-1)


def fetch_panel(whitened, panel_root, panel_first):
    candidate = lax.dynamic_slice_in_dim(whitened, panel_first, PP, 0)
    return spread(candidate, "block", panel_root)


def on_device(traces, valid, panel_owner, panel_start):
    channels, windows_here, segments, length = traces.shape
    bins = length // 2
    forward = forward_table(length)
    whitened = spectra_rows(
        traces.reshape(channels * windows_here * segments, length),
        valid.reshape(channels * windows_here * segments),
        forward,
    )
    whitened = whitened.reshape(channels, windows_here, segments, 2 * bins)
    pieces = []
    for panel in range(NP):
        pieces.append(fetch_panel(whitened, panel_owner[panel], panel_start[panel]))
    sources = jnp.concatenate(pieces, axis=0)
    groups = lax.axis_size("tm")
    inverse = inverse_table(length, 1.0 / math.sqrt(bins * windows_here * segments * groups))
    source_count = sources.shape[0]
    own_rows = whitened.reshape(channels, windows_here * segments, 2 * bins)
    source_rows = sources.reshape(source_count, windows_here * segments, 2 * bins)
    stacked = lax.psum_scatter(
        correlate(source_rows, own_rows), "tm", scatter_dimension=0, tiled=True
    )
    return jnp.dot(stacked, inverse, precision=lax.Precision.HIGHEST)


def edge_first(values, groups):
    return lax.ppermute(values, "tm", [(0, 1), (groups - 1, groups - 2)])


def whiten_kernel(rows_ref, forward_ref, mask_ref, out_ref):
    spectrum = jnp.dot(rows_ref[...], forward_ref[...], preferred_element_type=jnp.float32)
    energy = jnp.mean(spectrum * spectrum, axis=1, keepdims=True)
    scaled = spectrum * lax.rsqrt(energy + 1e-06) * mask_ref[...]
    out_ref[...] = scaled.astype(jnp.bfloat16).reshape(out_ref.shape)


def whiten_segments(rows, mask, forward, chunks):
    segments, channels, length = rows.shape
    width = channels // chunks
    return pl.pallas_call(
        whiten_kernel,
        grid=(segments,),
        in_specs=[
            pl.BlockSpec((None, channels, length), lambda m: (m, 0, 0)),
            pl.BlockSpec((length, length), lambda m: (0, 0)),
            pl.BlockSpec((None, channels, 1), lambda m: (m, 0, 0)),
        ],
        out_specs=pl.BlockSpec((chunks, None, width, length), lambda m: (0, m, 0, 0)),
        out_shape=jax.ShapeDtypeStruct((chunks, segments, width, length), jnp.bfloat16),
    )(rows, forward, mask)


LANES = 128
ROWS = 8


def cross_kernel(own_ref, src_ref, out_ref):
    segments = own_ref.shape[0]
    sources = src_ref.shape[1]
    rows = own_ref.shape[1]
    bins = own_ref.shape[-1] // 2

    def tile_body(tile, carry):
        re_lanes = pl.ds(pl.multiple_of(tile * LANES, LANES), LANES)
        im_lanes = pl.ds(pl.multiple_of(bins + tile * LANES, LANES), LANES)

        def step(m, acc):
            wr = own_ref[m, :, re_lanes].astype(jnp.float32)
            wi = own_ref[m, :, im_lanes].astype(jnp.float32)
            out = []
            for j in range(sources):
                sr = jnp.concatenate([src_ref[m, j, :, re_lanes]] * (rows // ROWS), axis=0)
                si = jnp.concatenate([src_ref[m, j, :, im_lanes]] * (rows // ROWS), axis=0)
                out.append(acc[2 * j] + (wr * sr + wi * si))
                out.append(acc[2 * j + 1] + (wi * sr - wr * si))
            return tuple(out)

        acc = tuple(jnp.zeros((rows, LANES), jnp.float32) for _ in range(2 * sources))
        acc = lax.fori_loop(0, segments, step, acc)
        for j in range(sources):
            out_ref[j, :, re_lanes] = acc[2 * j]
            out_ref[j, :, im_lanes] = acc[2 * j + 1]
        return carry

    lax.fori_loop(0, bins // LANES, tile_body, 0)


def cross_chunk(own, src):
    segments, width, length = own.shape
    sources = src.shape[1]
    step_rows = 2 * ROWS
    return pl.pallas_call(
        cross_kernel,
        grid=(width // step_rows,),
        in_specs=[
            pl.BlockSpec((segments, step_rows, length), lambda i: (0, i, 0)),
            pl.BlockSpec((segments, sources, ROWS, length), lambda i: (0, 0, 0, 0)),
        ],
        out_specs=pl.BlockSpec((sources, step_rows, length), lambda i: (0, i, 0)),
        out_shape=jax.ShapeDtypeStruct((sources, width, length), jnp.float32),
    )(own, src)


def butterfly_sum(values, axis):
    count = lax.axis_size(axis)
    step = 1
    while step < count:
        values = values + lax.ppermute(values, axis, [(b, b ^ step) for b in range(count)])
        step *= 2
    return values


def widen(values, length):
    segments, count = values.shape[0], values.shape[1]
    return jnp.broadcast_to(values.astype(jnp.float32)[:, :, None, :], (segments, count, ROWS, length))


def on_line(traces, valid, panel_owner, panel_start):
    channels, windows_here, segments, length = traces.shape
    bins = length // 2
    groups = lax.axis_size("tm")
    place = lax.axis_index("tm")
    chunks = 8
    width = channels // chunks
    seg_count = windows_here * segments
    forward = forward_table(length)
    rows = traces.reshape(channels, seg_count, length).transpose(1, 0, 2)
    mask = valid.reshape(channels, seg_count).transpose(1, 0).astype(jnp.float32)[:, :, None]
    whitened = whiten_segments(rows, mask, forward, chunks)
    block_place = lax.axis_index("block")
    pieces = []
    for panel in range(NP):
        first = panel_start[panel]
        chunk_of = first // width
        candidate = lax.dynamic_slice_in_dim(
            lax.dynamic_index_in_dim(whitened, chunk_of, 0, keepdims=False), first - chunk_of * width, PP, 1
        )
        pieces.append(jnp.where(block_place == panel_owner[panel], candidate, 0).astype(candidate.dtype))
    sources = butterfly_sum(jnp.concatenate(pieces, axis=1), "block")
    source_count = sources.shape[1]
    per_group = source_count // groups
    half = source_count // 2
    first_half = place < groups // 2
    turned = jnp.concatenate(
        [sources[:, source_count - per_group:], sources[:, half:source_count - per_group]], axis=1
    )
    far = jnp.where(first_half, turned, sources[:, :half])
    near = jnp.where(first_half, sources[:, :half], turned)
    inverse = inverse_table(length, 1.0 / math.sqrt(bins * seg_count * groups))
    is_edge = jnp.logical_or(place == 0, place == groups - 1)
    far_wide, near_wide = widen(far, length), widen(near, length)
    outs = []
    last_edge = None
    last_middle = None
    for chunk in range(chunks):
        own = whitened[chunk]
        far_part = cross_chunk(own, far_wide)
        near_part = cross_chunk(own, near_wide)
        edge_out = jnp.concatenate([far_part, near_part[per_group:]], axis=0).astype(jnp.bfloat16)
        if last_edge is not None:
            edge_out, _ = lax.optimization_barrier((edge_out, last_edge))
        edge_in = edge_first(edge_out, groups)
        last_edge = edge_in
        far_total = far_part + edge_in[:half].astype(jnp.float32)
        if last_middle is not None:
            far_total, _ = lax.optimization_barrier((far_total, last_middle))
        got = lax.ppermute(far_total, "tm", [(1, 2), (2, 1)])
        last_middle = got
        low = near_part[:per_group] + got[:per_group]
        high = near_part[per_group:] + edge_in[half:].astype(jnp.float32) + got[per_group:]
        back = lax.ppermute(low, "tm", [(1, 0), (2, 3)])
        final = jnp.where(is_edge, near_part[:per_group] + back, high)
        outs.append(jnp.dot(final, inverse, precision=lax.Precision.HIGHEST))
    return jnp.concatenate(outs, axis=1)


def solution(mesh):
    in_specs = (P("block", "tm", None, None), P("block", "tm", None), P(), P())
    out_specs = P("tm", "block", None)
    body = on_line if mesh.shape["tm"] == 4 else on_device
    return jax.shard_map(
        body, mesh=mesh, in_specs=in_specs, out_specs=out_specs, check_vma=False
    )
```

```python
import math

import jax
import jax.numpy as jnp
from jax import lax
from jax.sharding import PartitionSpec as P
from jax.experimental import pallas as pl
from jax.experimental.pallas import tpu as pltpu

PP = 4
NP = 4


def spread(value, axis, source):
    kept = jnp.where(lax.axis_index(axis) == source, value, 0).astype(value.dtype)
    return lax.psum(kept, axis)


def forward_table(length):
    sample = jnp.arange(length, dtype=jnp.int32)
    bin_index = jnp.arange(length // 2, dtype=jnp.int32)
    angles = (sample[:, None] * bin_index[None, :] % length).astype(jnp.float32) * (
        2.0 * math.pi / length
    )
    return jnp.concatenate([jnp.cos(angles), -jnp.sin(angles)], axis=1).astype(jnp.bfloat16)


def inverse_table(length, factor):
    bin_index = jnp.arange(length // 2, dtype=jnp.int32)
    lag_index = jnp.arange(length, dtype=jnp.int32)
    angles = (bin_index[:, None] * lag_index[None, :] % length).astype(jnp.float32) * (
        2.0 * math.pi / length
    )
    weight = jnp.where(bin_index == 0, 1.0, 2.0).astype(jnp.float32)[:, None] * factor
    return jnp.concatenate([weight * jnp.cos(angles), -weight * jnp.sin(angles)], axis=0)


def whiten(segment_rows, valid_mask, forward):
    spectrum = jnp.dot(segment_rows, forward, preferred_element_type=jnp.float32)
    energy = jnp.mean(spectrum * spectrum, axis=1, keepdims=True)
    return (spectrum * lax.rsqrt(energy + 1e-06) * valid_mask[:, None].astype(jnp.float32)).astype(
        jnp.bfloat16
    )


def spectra_rows(segment_rows, valid_mask, forward):
    return whiten(segment_rows, valid_mask, forward)


def correlate(left, right):
    bins = left.shape[-1] // 2
    left_both = jnp.concatenate([left[..., :bins], left[..., bins:]], axis=1)
    right_both = jnp.concatenate([right[..., :bins], right[..., bins:]], axis=1)
    right_turn = jnp.concatenate([right[..., bins:], -right[..., :bins]], axis=1)
    real_part = jnp.einsum(
        "jmk,imk->jik", left_both, right_both, preferred_element_type=jnp.float32
    )
    imag_part = jnp.einsum(
        "jmk,imk->jik", left_both, right_turn, preferred_element_type=jnp.float32
    )
    return jnp.concatenate([real_part, imag_part], axis=-1)


def fetch_panel(whitened, panel_root, panel_first):
    candidate = lax.dynamic_slice_in_dim(whitened, panel_first, PP, 0)
    return spread(candidate, "block", panel_root)


def on_device(traces, valid, panel_owner, panel_start):
    channels, windows_here, segments, length = traces.shape
    bins = length // 2
    forward = forward_table(length)
    whitened = spectra_rows(
        traces.reshape(channels * windows_here * segments, length),
        valid.reshape(channels * windows_here * segments),
        forward,
    )
    whitened = whitened.reshape(channels, windows_here, segments, 2 * bins)
    pieces = []
    for panel in range(NP):
        pieces.append(fetch_panel(whitened, panel_owner[panel], panel_start[panel]))
    sources = jnp.concatenate(pieces, axis=0)
    groups = lax.axis_size("tm")
    inverse = inverse_table(length, 1.0 / math.sqrt(bins * windows_here * segments * groups))
    source_count = sources.shape[0]
    own_rows = whitened.reshape(channels, windows_here * segments, 2 * bins)
    source_rows = sources.reshape(source_count, windows_here * segments, 2 * bins)
    stacked = lax.psum_scatter(
        correlate(source_rows, own_rows), "tm", scatter_dimension=0, tiled=True
    )
    return jnp.dot(stacked, inverse, precision=lax.Precision.HIGHEST)


def edge_first(values, groups):
    return lax.ppermute(values, "tm", [(0, 1), (groups - 1, groups - 2)])


def whiten_kernel(rows_ref, forward_ref, mask_ref, out_ref):
    spectrum = jnp.dot(rows_ref[...], forward_ref[...], preferred_element_type=jnp.float32)
    energy = jnp.mean(spectrum * spectrum, axis=1, keepdims=True)
    scaled = spectrum * lax.rsqrt(energy + 1e-06) * mask_ref[...]
    out_ref[...] = scaled.astype(jnp.bfloat16).reshape(out_ref.shape)


def whiten_segments(rows, mask, forward, chunks):
    segments, channels, length = rows.shape
    width = channels // chunks
    return pl.pallas_call(
        whiten_kernel,
        grid=(segments,),
        in_specs=[
            pl.BlockSpec((None, channels, length), lambda m: (m, 0, 0)),
            pl.BlockSpec((length, length), lambda m: (0, 0)),
            pl.BlockSpec((None, channels, 1), lambda m: (m, 0, 0)),
        ],
        out_specs=pl.BlockSpec((chunks, None, width, length), lambda m: (0, m, 0, 0)),
        out_shape=jax.ShapeDtypeStruct((chunks, segments, width, length), jnp.bfloat16),
    )(rows, forward, mask)


LANES = 128
ROWS = 8


def cross_kernel(own_ref, src_ref, out_ref):
    segments = own_ref.shape[0]
    sources = src_ref.shape[1]
    rows = own_ref.shape[1]
    bins = own_ref.shape[-1] // 2

    def tile_body(tile, carry):
        re_lanes = pl.ds(pl.multiple_of(tile * LANES, LANES), LANES)
        im_lanes = pl.ds(pl.multiple_of(bins + tile * LANES, LANES), LANES)

        def step(m, acc):
            wr = own_ref[m, :, re_lanes].astype(jnp.float32)
            wi = own_ref[m, :, im_lanes].astype(jnp.float32)
            out = []
            for j in range(sources):
                sr = jnp.concatenate([src_ref[m, j, :, re_lanes]] * (rows // ROWS), axis=0)
                si = jnp.concatenate([src_ref[m, j, :, im_lanes]] * (rows // ROWS), axis=0)
                out.append(acc[2 * j] + (wr * sr + wi * si))
                out.append(acc[2 * j + 1] + (wi * sr - wr * si))
            return tuple(out)

        acc = tuple(jnp.zeros((rows, LANES), jnp.float32) for _ in range(2 * sources))
        acc = lax.fori_loop(0, segments, step, acc)
        for j in range(sources):
            out_ref[j, :, re_lanes] = acc[2 * j]
            out_ref[j, :, im_lanes] = acc[2 * j + 1]
        return carry

    lax.fori_loop(0, bins // LANES, tile_body, 0)


def cross_chunk(own, src):
    segments, width, length = own.shape
    sources = src.shape[1]
    step_rows = 2 * ROWS
    return pl.pallas_call(
        cross_kernel,
        grid=(width // step_rows,),
        in_specs=[
            pl.BlockSpec((segments, step_rows, length), lambda i: (0, i, 0)),
            pl.BlockSpec((segments, sources, ROWS, length), lambda i: (0, 0, 0, 0)),
        ],
        out_specs=pl.BlockSpec((sources, step_rows, length), lambda i: (0, i, 0)),
        out_shape=jax.ShapeDtypeStruct((sources, width, length), jnp.float32),
    )(own, src)


def butterfly_sum(values, axis):
    count = lax.axis_size(axis)
    step = 1
    while step < count:
        values = values + lax.ppermute(values, axis, [(b, b ^ step) for b in range(count)])
        step *= 2
    return values


def widen(values, length):
    segments, count = values.shape[0], values.shape[1]
    return jnp.broadcast_to(values.astype(jnp.float32)[:, :, None, :], (segments, count, ROWS, length))


def on_line(traces, valid, panel_owner, panel_start):
    channels, windows_here, segments, length = traces.shape
    bins = length // 2
    groups = lax.axis_size("tm")
    place = lax.axis_index("tm")
    chunks = 8
    width = channels // chunks
    seg_count = windows_here * segments
    forward = forward_table(length)
    rows = traces.reshape(channels, seg_count, length).transpose(1, 0, 2)
    mask = valid.reshape(channels, seg_count).transpose(1, 0).astype(jnp.float32)[:, :, None]
    whitened = whiten_segments(rows, mask, forward, chunks)
    block_place = lax.axis_index("block")
    pieces = []
    for panel in range(NP):
        first = panel_start[panel]
        chunk_of = first // width
        candidate = lax.dynamic_slice_in_dim(
            lax.dynamic_index_in_dim(whitened, chunk_of, 0, keepdims=False), first - chunk_of * width, PP, 1
        )
        pieces.append(jnp.where(block_place == panel_owner[panel], candidate, 0).astype(candidate.dtype))
    sources = butterfly_sum(jnp.concatenate(pieces, axis=1), "block")
    source_count = sources.shape[1]
    per_group = source_count // groups
    half = source_count // 2
    first_half = place < groups // 2
    turned = jnp.concatenate(
        [sources[:, source_count - per_group:], sources[:, half:source_count - per_group]], axis=1
    )
    far = jnp.where(first_half, turned, sources[:, :half])
    near = jnp.where(first_half, sources[:, :half], turned)
    inverse = inverse_table(length, 1.0 / math.sqrt(bins * seg_count * groups))
    is_edge = jnp.logical_or(place == 0, place == groups - 1)
    far_wide, near_wide = widen(far, length), widen(near, length)
    outs = []
    last_edge = None
    last_middle = None
    for chunk in range(chunks):
        own = whitened[chunk]
        far_part = cross_chunk(own, far_wide)
        near_part = cross_chunk(own, near_wide)
        edge_out = jnp.concatenate([far_part, near_part[per_group:]], axis=0).astype(jnp.bfloat16)
        if last_edge is not None:
            edge_out, _ = lax.optimization_barrier((edge_out, last_edge))
        edge_in = edge_first(edge_out, groups)
        last_edge = edge_in
        far_total = far_part + edge_in[:half].astype(jnp.float32)
        if last_middle is not None:
            far_total, _ = lax.optimization_barrier((far_total, last_middle))
        got = lax.ppermute(far_total.astype(jnp.bfloat16), "tm", [(1, 2), (2, 1)])
        last_middle = got
        got = got.astype(jnp.float32)
        low = near_part[:per_group] + got[:per_group]
        high = near_part[per_group:] + edge_in[half:].astype(jnp.float32) + got[per_group:]
        back = lax.ppermute(low, "tm", [(1, 0), (2, 3)])
        final = jnp.where(is_edge, near_part[:per_group] + back, high)
        outs.append(jnp.dot(final, inverse, precision=lax.Precision.HIGHEST))
    return jnp.concatenate(outs, axis=1)


def solution(mesh):
    in_specs = (P("block", "tm", None, None), P("block", "tm", None), P(), P())
    out_specs = P("tm", "block", None)
    body = on_line if mesh.shape["tm"] == 4 else on_device
    return jax.shard_map(
        body, mesh=mesh, in_specs=in_specs, out_specs=out_specs, check_vma=False
    )
```

```python
import math

import jax
import jax.numpy as jnp
from jax import lax
from jax.sharding import PartitionSpec as P
from jax.experimental import pallas as pl
from jax.experimental.pallas import tpu as pltpu

PP = 4
NP = 4


def spread(value, axis, source):
    kept = jnp.where(lax.axis_index(axis) == source, value, 0).astype(value.dtype)
    return lax.psum(kept, axis)


def forward_table(length):
    sample = jnp.arange(length, dtype=jnp.int32)
    bin_index = jnp.arange(length // 2, dtype=jnp.int32)
    angles = (sample[:, None] * bin_index[None, :] % length).astype(jnp.float32) * (
        2.0 * math.pi / length
    )
    return jnp.concatenate([jnp.cos(angles), -jnp.sin(angles)], axis=1).astype(jnp.bfloat16)


def inverse_table(length, factor):
    bin_index = jnp.arange(length // 2, dtype=jnp.int32)
    lag_index = jnp.arange(length, dtype=jnp.int32)
    angles = (bin_index[:, None] * lag_index[None, :] % length).astype(jnp.float32) * (
        2.0 * math.pi / length
    )
    weight = jnp.where(bin_index == 0, 1.0, 2.0).astype(jnp.float32)[:, None] * factor
    return jnp.concatenate([weight * jnp.cos(angles), -weight * jnp.sin(angles)], axis=0)


def whiten(segment_rows, valid_mask, forward):
    spectrum = jnp.dot(segment_rows, forward, preferred_element_type=jnp.float32)
    energy = jnp.mean(spectrum * spectrum, axis=1, keepdims=True)
    return (spectrum * lax.rsqrt(energy + 1e-06) * valid_mask[:, None].astype(jnp.float32)).astype(
        jnp.bfloat16
    )


def spectra_rows(segment_rows, valid_mask, forward):
    return whiten(segment_rows, valid_mask, forward)


def correlate(left, right):
    bins = left.shape[-1] // 2
    left_both = jnp.concatenate([left[..., :bins], left[..., bins:]], axis=1)
    right_both = jnp.concatenate([right[..., :bins], right[..., bins:]], axis=1)
    right_turn = jnp.concatenate([right[..., bins:], -right[..., :bins]], axis=1)
    real_part = jnp.einsum(
        "jmk,imk->jik", left_both, right_both, preferred_element_type=jnp.float32
    )
    imag_part = jnp.einsum(
        "jmk,imk->jik", left_both, right_turn, preferred_element_type=jnp.float32
    )
    return jnp.concatenate([real_part, imag_part], axis=-1)


def fetch_panel(whitened, panel_root, panel_first):
    candidate = lax.dynamic_slice_in_dim(whitened, panel_first, PP, 0)
    return spread(candidate, "block", panel_root)


def on_device(traces, valid, panel_owner, panel_start):
    channels, windows_here, segments, length = traces.shape
    bins = length // 2
    forward = forward_table(length)
    whitened = spectra_rows(
        traces.reshape(channels * windows_here * segments, length),
        valid.reshape(channels * windows_here * segments),
        forward,
    )
    whitened = whitened.reshape(channels, windows_here, segments, 2 * bins)
    pieces = []
    for panel in range(NP):
        pieces.append(fetch_panel(whitened, panel_owner[panel], panel_start[panel]))
    sources = jnp.concatenate(pieces, axis=0)
    groups = lax.axis_size("tm")
    inverse = inverse_table(length, 1.0 / math.sqrt(bins * windows_here * segments * groups))
    source_count = sources.shape[0]
    own_rows = whitened.reshape(channels, windows_here * segments, 2 * bins)
    source_rows = sources.reshape(source_count, windows_here * segments, 2 * bins)
    stacked = lax.psum_scatter(
        correlate(source_rows, own_rows), "tm", scatter_dimension=0, tiled=True
    )
    return jnp.dot(stacked, inverse, precision=lax.Precision.HIGHEST)


def edge_first(values, groups):
    return lax.ppermute(values, "tm", [(0, 1), (groups - 1, groups - 2)])


def whiten_kernel(rows_ref, forward_ref, mask_ref, out_ref):
    spectrum = jnp.dot(rows_ref[...], forward_ref[...], preferred_element_type=jnp.float32)
    energy = jnp.mean(spectrum * spectrum, axis=1, keepdims=True)
    scaled = spectrum * lax.rsqrt(energy + 1e-06) * mask_ref[...]
    out_ref[...] = scaled.astype(jnp.bfloat16).reshape(out_ref.shape)


def whiten_segments(rows, mask, forward, chunks):
    segments, channels, length = rows.shape
    width = channels // chunks
    return pl.pallas_call(
        whiten_kernel,
        grid=(segments,),
        in_specs=[
            pl.BlockSpec((None, channels, length), lambda m: (m, 0, 0)),
            pl.BlockSpec((length, length), lambda m: (0, 0)),
            pl.BlockSpec((None, channels, 1), lambda m: (m, 0, 0)),
        ],
        out_specs=pl.BlockSpec((chunks, None, width, length), lambda m: (0, m, 0, 0)),
        out_shape=jax.ShapeDtypeStruct((chunks, segments, width, length), jnp.bfloat16),
    )(rows, forward, mask)


LANES = 128
ROWS = 8


def cross_kernel(own_ref, src_ref, out_ref):
    segments = own_ref.shape[0]
    sources = src_ref.shape[1]
    rows = own_ref.shape[1]
    bins = own_ref.shape[-1] // 2

    def tile_body(tile, carry):
        re_lanes = pl.ds(pl.multiple_of(tile * LANES, LANES), LANES)
        im_lanes = pl.ds(pl.multiple_of(bins + tile * LANES, LANES), LANES)

        def step(m, acc):
            wr = own_ref[m, :, re_lanes].astype(jnp.float32)
            wi = own_ref[m, :, im_lanes].astype(jnp.float32)
            out = []
            for j in range(sources):
                sr = jnp.concatenate([src_ref[m, j, :, re_lanes]] * (rows // ROWS), axis=0)
                si = jnp.concatenate([src_ref[m, j, :, im_lanes]] * (rows // ROWS), axis=0)
                out.append(acc[2 * j] + (wr * sr + wi * si))
                out.append(acc[2 * j + 1] + (wi * sr - wr * si))
            return tuple(out)

        acc = tuple(jnp.zeros((rows, LANES), jnp.float32) for _ in range(2 * sources))
        acc = lax.fori_loop(0, segments, step, acc)
        for j in range(sources):
            out_ref[j, :, re_lanes] = acc[2 * j]
            out_ref[j, :, im_lanes] = acc[2 * j + 1]
        return carry

    lax.fori_loop(0, bins // LANES, tile_body, 0)


def cross_chunk(own, src):
    segments, width, length = own.shape
    sources = src.shape[1]
    step_rows = 2 * ROWS
    return pl.pallas_call(
        cross_kernel,
        grid=(width // step_rows,),
        in_specs=[
            pl.BlockSpec((segments, step_rows, length), lambda i: (0, i, 0)),
            pl.BlockSpec((segments, sources, ROWS, length), lambda i: (0, 0, 0, 0)),
        ],
        out_specs=pl.BlockSpec((sources, step_rows, length), lambda i: (0, i, 0)),
        out_shape=jax.ShapeDtypeStruct((sources, width, length), jnp.float32),
    )(own, src)


def butterfly_sum(values, axis):
    count = lax.axis_size(axis)
    step = 1
    while step < count:
        values = values + lax.ppermute(values, axis, [(b, b ^ step) for b in range(count)])
        step *= 2
    return values


def widen(values, length):
    segments, count = values.shape[0], values.shape[1]
    return jnp.broadcast_to(values.astype(jnp.float32)[:, :, None, :], (segments, count, ROWS, length))


def on_line(traces, valid, panel_owner, panel_start):
    channels, windows_here, segments, length = traces.shape
    bins = length // 2
    groups = lax.axis_size("tm")
    place = lax.axis_index("tm")
    chunks = 8
    width = channels // chunks
    seg_count = windows_here * segments
    forward = forward_table(length)
    rows = traces.reshape(channels, seg_count, length).transpose(1, 0, 2)
    mask = valid.reshape(channels, seg_count).transpose(1, 0).astype(jnp.float32)[:, :, None]
    whitened = whiten_segments(rows, mask, forward, chunks)
    block_place = lax.axis_index("block")
    pieces = []
    for panel in range(NP):
        first = panel_start[panel]
        chunk_of = first // width
        candidate = lax.dynamic_slice_in_dim(
            lax.dynamic_index_in_dim(whitened, chunk_of, 0, keepdims=False), first - chunk_of * width, PP, 1
        )
        pieces.append(jnp.where(block_place == panel_owner[panel], candidate, 0).astype(candidate.dtype))
    sources = butterfly_sum(jnp.concatenate(pieces, axis=1), "block")
    source_count = sources.shape[1]
    per_group = source_count // groups
    half = source_count // 2
    first_half = place < groups // 2
    turned = jnp.concatenate(
        [sources[:, source_count - per_group:], sources[:, half:source_count - per_group]], axis=1
    )
    far = jnp.where(first_half, turned, sources[:, :half])
    near = jnp.where(first_half, sources[:, :half], turned)
    inverse = inverse_table(length, 1.0 / math.sqrt(bins * seg_count * groups))
    is_edge = jnp.logical_or(place == 0, place == groups - 1)
    far_wide, near_wide = widen(far, length), widen(near, length)
    outs = []
    for chunk in range(chunks):
        own = whitened[chunk]
        far_part = cross_chunk(own, far_wide)
        near_part = cross_chunk(own, near_wide)
        edge_out = jnp.concatenate([far_part, near_part[per_group:]], axis=0).astype(jnp.bfloat16)
        edge_in = edge_first(edge_out, groups)
        far_total = far_part + edge_in[:half].astype(jnp.float32)
        got = lax.ppermute(far_total.astype(jnp.bfloat16), "tm", [(1, 2), (2, 1)])
        got = got.astype(jnp.float32)
        low = near_part[:per_group] + got[:per_group]
        high = near_part[per_group:] + edge_in[half:].astype(jnp.float32) + got[per_group:]
        back = lax.ppermute(low, "tm", [(1, 0), (2, 3)])
        final = jnp.where(is_edge, near_part[:per_group] + back, high)
        outs.append(jnp.dot(final, inverse, precision=lax.Precision.HIGHEST))
    return jnp.concatenate(outs, axis=1)


def solution(mesh):
    in_specs = (P("block", "tm", None, None), P("block", "tm", None), P(), P())
    out_specs = P("tm", "block", None)
    body = on_line if mesh.shape["tm"] == 4 else on_device
    return jax.shard_map(
        body, mesh=mesh, in_specs=in_specs, out_specs=out_specs, check_vma=False
    )
```

```python
import math

import jax
import jax.numpy as jnp
from jax import lax
from jax.sharding import PartitionSpec as P
from jax.experimental import pallas as pl
from jax.experimental.pallas import tpu as pltpu

PP = 4
NP = 4


def spread(value, axis, source):
    kept = jnp.where(lax.axis_index(axis) == source, value, 0).astype(value.dtype)
    return lax.psum(kept, axis)


def forward_table(length):
    sample = jnp.arange(length, dtype=jnp.int32)
    bin_index = jnp.arange(length // 2, dtype=jnp.int32)
    angles = (sample[:, None] * bin_index[None, :] % length).astype(jnp.float32) * (
        2.0 * math.pi / length
    )
    return jnp.concatenate([jnp.cos(angles), -jnp.sin(angles)], axis=1).astype(jnp.bfloat16)


def inverse_table(length, factor):
    bin_index = jnp.arange(length // 2, dtype=jnp.int32)
    lag_index = jnp.arange(length, dtype=jnp.int32)
    angles = (bin_index[:, None] * lag_index[None, :] % length).astype(jnp.float32) * (
        2.0 * math.pi / length
    )
    weight = jnp.where(bin_index == 0, 1.0, 2.0).astype(jnp.float32)[:, None] * factor
    return jnp.concatenate([weight * jnp.cos(angles), -weight * jnp.sin(angles)], axis=0)


def whiten(segment_rows, valid_mask, forward):
    spectrum = jnp.dot(segment_rows, forward, preferred_element_type=jnp.float32)
    energy = jnp.mean(spectrum * spectrum, axis=1, keepdims=True)
    return (spectrum * lax.rsqrt(energy + 1e-06) * valid_mask[:, None].astype(jnp.float32)).astype(
        jnp.bfloat16
    )


def spectra_rows(segment_rows, valid_mask, forward):
    return whiten(segment_rows, valid_mask, forward)


def correlate(left, right):
    bins = left.shape[-1] // 2
    left_both = jnp.concatenate([left[..., :bins], left[..., bins:]], axis=1)
    right_both = jnp.concatenate([right[..., :bins], right[..., bins:]], axis=1)
    right_turn = jnp.concatenate([right[..., bins:], -right[..., :bins]], axis=1)
    real_part = jnp.einsum(
        "jmk,imk->jik", left_both, right_both, preferred_element_type=jnp.float32
    )
    imag_part = jnp.einsum(
        "jmk,imk->jik", left_both, right_turn, preferred_element_type=jnp.float32
    )
    return jnp.concatenate([real_part, imag_part], axis=-1)


def fetch_panel(whitened, panel_root, panel_first):
    candidate = lax.dynamic_slice_in_dim(whitened, panel_first, PP, 0)
    return spread(candidate, "block", panel_root)


def on_device(traces, valid, panel_owner, panel_start):
    channels, windows_here, segments, length = traces.shape
    bins = length // 2
    forward = forward_table(length)
    whitened = spectra_rows(
        traces.reshape(channels * windows_here * segments, length),
        valid.reshape(channels * windows_here * segments),
        forward,
    )
    whitened = whitened.reshape(channels, windows_here, segments, 2 * bins)
    pieces = []
    for panel in range(NP):
        pieces.append(fetch_panel(whitened, panel_owner[panel], panel_start[panel]))
    sources = jnp.concatenate(pieces, axis=0)
    groups = lax.axis_size("tm")
    inverse = inverse_table(length, 1.0 / math.sqrt(bins * windows_here * segments * groups))
    source_count = sources.shape[0]
    own_rows = whitened.reshape(channels, windows_here * segments, 2 * bins)
    source_rows = sources.reshape(source_count, windows_here * segments, 2 * bins)
    stacked = lax.psum_scatter(
        correlate(source_rows, own_rows), "tm", scatter_dimension=0, tiled=True
    )
    return jnp.dot(stacked, inverse, precision=lax.Precision.HIGHEST)


def edge_first(values, groups):
    return lax.ppermute(values, "tm", [(0, 1), (groups - 1, groups - 2)])


def whiten_kernel(rows_ref, forward_ref, mask_ref, out_ref):
    spectrum = jnp.dot(rows_ref[...], forward_ref[...], preferred_element_type=jnp.float32)
    energy = jnp.mean(spectrum * spectrum, axis=1, keepdims=True)
    scaled = spectrum * lax.rsqrt(energy + 1e-06) * mask_ref[...]
    out_ref[...] = scaled.astype(jnp.bfloat16).reshape(out_ref.shape)


def whiten_segments(rows, mask, forward, chunks):
    segments, channels, length = rows.shape
    width = channels // chunks
    return pl.pallas_call(
        whiten_kernel,
        grid=(segments,),
        in_specs=[
            pl.BlockSpec((None, channels, length), lambda m: (m, 0, 0)),
            pl.BlockSpec((length, length), lambda m: (0, 0)),
            pl.BlockSpec((None, channels, 1), lambda m: (m, 0, 0)),
        ],
        out_specs=pl.BlockSpec((chunks, None, width, length), lambda m: (0, m, 0, 0)),
        out_shape=jax.ShapeDtypeStruct((chunks, segments, width, length), jnp.bfloat16),
    )(rows, forward, mask)


LANES = 128
ROWS = 8


def cross_kernel(own_ref, src_ref, out_ref):
    segments = own_ref.shape[0]
    sources = src_ref.shape[1]
    rows = own_ref.shape[1]
    bins = own_ref.shape[-1] // 2

    def tile_body(tile, carry):
        re_lanes = pl.ds(pl.multiple_of(tile * LANES, LANES), LANES)
        im_lanes = pl.ds(pl.multiple_of(bins + tile * LANES, LANES), LANES)

        def step(m, acc):
            wr = own_ref[m, :, re_lanes].astype(jnp.float32)
            wi = own_ref[m, :, im_lanes].astype(jnp.float32)
            out = []
            for j in range(sources):
                sr = jnp.concatenate([src_ref[m, j, :, re_lanes]] * (rows // ROWS), axis=0)
                si = jnp.concatenate([src_ref[m, j, :, im_lanes]] * (rows // ROWS), axis=0)
                out.append(acc[2 * j] + (wr * sr + wi * si))
                out.append(acc[2 * j + 1] + (wi * sr - wr * si))
            return tuple(out)

        acc = tuple(jnp.zeros((rows, LANES), jnp.float32) for _ in range(2 * sources))
        acc = lax.fori_loop(0, segments, step, acc)
        for j in range(sources):
            out_ref[j, :, re_lanes] = acc[2 * j]
            out_ref[j, :, im_lanes] = acc[2 * j + 1]
        return carry

    lax.fori_loop(0, bins // LANES, tile_body, 0)


def cross_chunk(own, src):
    segments, width, length = own.shape
    sources = src.shape[1]
    step_rows = 2 * ROWS
    return pl.pallas_call(
        cross_kernel,
        grid=(width // step_rows,),
        in_specs=[
            pl.BlockSpec((segments, step_rows, length), lambda i: (0, i, 0)),
            pl.BlockSpec((segments, sources, ROWS, length), lambda i: (0, 0, 0, 0)),
        ],
        out_specs=pl.BlockSpec((sources, step_rows, length), lambda i: (0, i, 0)),
        out_shape=jax.ShapeDtypeStruct((sources, width, length), jnp.float32),
    )(own, src)


def butterfly_sum(values, axis):
    count = lax.axis_size(axis)
    step = 1
    while step < count:
        values = values + lax.ppermute(values, axis, [(b, b ^ step) for b in range(count)])
        step *= 2
    return values


def widen(values, length):
    segments, count = values.shape[0], values.shape[1]
    return jnp.broadcast_to(values.astype(jnp.float32)[:, :, None, :], (segments, count, ROWS, length))


def on_line(traces, valid, panel_owner, panel_start):
    channels, windows_here, segments, length = traces.shape
    bins = length // 2
    groups = lax.axis_size("tm")
    place = lax.axis_index("tm")
    chunks = 8
    width = channels // chunks
    seg_count = windows_here * segments
    forward = forward_table(length)
    rows = traces.reshape(channels, seg_count, length).transpose(1, 0, 2)
    mask = valid.reshape(channels, seg_count).transpose(1, 0).astype(jnp.float32)[:, :, None]
    whitened = whiten_segments(rows, mask, forward, chunks)
    block_place = lax.axis_index("block")
    pieces = []
    for panel in range(NP):
        first = panel_start[panel]
        chunk_of = first // width
        candidate = lax.dynamic_slice_in_dim(
            lax.dynamic_index_in_dim(whitened, chunk_of, 0, keepdims=False), first - chunk_of * width, PP, 1
        )
        pieces.append(jnp.where(block_place == panel_owner[panel], candidate, 0).astype(candidate.dtype))
    sources = butterfly_sum(jnp.concatenate(pieces, axis=1), "block")
    source_count = sources.shape[1]
    per_group = source_count // groups
    half = source_count // 2
    first_half = place < groups // 2
    turned = jnp.concatenate(
        [sources[:, source_count - per_group:], sources[:, half:source_count - per_group]], axis=1
    )
    far = jnp.where(first_half, turned, sources[:, :half])
    near = jnp.where(first_half, sources[:, :half], turned)
    inverse = inverse_table(length, 1.0 / math.sqrt(bins * seg_count * groups))
    is_edge = jnp.logical_or(place == 0, place == groups - 1)
    far_wide, near_wide = widen(far, length), widen(near, length)
    outs = []
    arrived = []
    for chunk in range(chunks):
        own = whitened[chunk]
        if chunk >= 2:
            own, _ = lax.optimization_barrier((own, arrived[chunk - 2]))
        far_part = cross_chunk(own, far_wide)
        near_part = cross_chunk(own, near_wide)
        edge_out = jnp.concatenate([far_part, near_part[per_group:]], axis=0).astype(jnp.bfloat16)
        if arrived:
            edge_out, _ = lax.optimization_barrier((edge_out, arrived[-1]))
        edge_in = edge_first(edge_out, groups)
        arrived.append(edge_in)
        far_total = far_part + edge_in[:half].astype(jnp.float32)
        got = lax.ppermute(far_total.astype(jnp.bfloat16), "tm", [(1, 2), (2, 1)]).astype(jnp.float32)
        low = near_part[:per_group] + got[:per_group]
        high = near_part[per_group:] + edge_in[half:].astype(jnp.float32) + got[per_group:]
        back = lax.ppermute(low, "tm", [(1, 0), (2, 3)])
        final = jnp.where(is_edge, near_part[:per_group] + back, high)
        outs.append(jnp.dot(final, inverse, precision=lax.Precision.HIGHEST))
    return jnp.concatenate(outs, axis=1)


def solution(mesh):
    in_specs = (P("block", "tm", None, None), P("block", "tm", None), P(), P())
    out_specs = P("tm", "block", None)
    body = on_line if mesh.shape["tm"] == 4 else on_device
    return jax.shard_map(
        body, mesh=mesh, in_specs=in_specs, out_specs=out_specs, check_vma=False
    )
```

```python
import math

import jax
import jax.numpy as jnp
from jax import lax
from jax.sharding import PartitionSpec as P
from jax.experimental import pallas as pl
from jax.experimental.pallas import tpu as pltpu

PP = 4
NP = 4


def spread(value, axis, source):
    kept = jnp.where(lax.axis_index(axis) == source, value, 0).astype(value.dtype)
    return lax.psum(kept, axis)


def forward_table(length):
    sample = jnp.arange(length, dtype=jnp.int32)
    bin_index = jnp.arange(length // 2, dtype=jnp.int32)
    angles = (sample[:, None] * bin_index[None, :] % length).astype(jnp.float32) * (
        2.0 * math.pi / length
    )
    return jnp.concatenate([jnp.cos(angles), -jnp.sin(angles)], axis=1).astype(jnp.bfloat16)


def inverse_table(length, factor):
    bin_index = jnp.arange(length // 2, dtype=jnp.int32)
    lag_index = jnp.arange(length, dtype=jnp.int32)
    angles = (bin_index[:, None] * lag_index[None, :] % length).astype(jnp.float32) * (
        2.0 * math.pi / length
    )
    weight = jnp.where(bin_index == 0, 1.0, 2.0).astype(jnp.float32)[:, None] * factor
    return jnp.concatenate([weight * jnp.cos(angles), -weight * jnp.sin(angles)], axis=0)


def whiten(segment_rows, valid_mask, forward):
    spectrum = jnp.dot(segment_rows, forward, preferred_element_type=jnp.float32)
    energy = jnp.mean(spectrum * spectrum, axis=1, keepdims=True)
    return (spectrum * lax.rsqrt(energy + 1e-06) * valid_mask[:, None].astype(jnp.float32)).astype(
        jnp.bfloat16
    )


def spectra_rows(segment_rows, valid_mask, forward):
    return whiten(segment_rows, valid_mask, forward)


def correlate(left, right):
    bins = left.shape[-1] // 2
    left_both = jnp.concatenate([left[..., :bins], left[..., bins:]], axis=1)
    right_both = jnp.concatenate([right[..., :bins], right[..., bins:]], axis=1)
    right_turn = jnp.concatenate([right[..., bins:], -right[..., :bins]], axis=1)
    real_part = jnp.einsum(
        "jmk,imk->jik", left_both, right_both, preferred_element_type=jnp.float32
    )
    imag_part = jnp.einsum(
        "jmk,imk->jik", left_both, right_turn, preferred_element_type=jnp.float32
    )
    return jnp.concatenate([real_part, imag_part], axis=-1)


def fetch_panel(whitened, panel_root, panel_first):
    candidate = lax.dynamic_slice_in_dim(whitened, panel_first, PP, 0)
    return spread(candidate, "block", panel_root)


def on_device(traces, valid, panel_owner, panel_start):
    channels, windows_here, segments, length = traces.shape
    bins = length // 2
    forward = forward_table(length)
    whitened = spectra_rows(
        traces.reshape(channels * windows_here * segments, length),
        valid.reshape(channels * windows_here * segments),
        forward,
    )
    whitened = whitened.reshape(channels, windows_here, segments, 2 * bins)
    pieces = []
    for panel in range(NP):
        pieces.append(fetch_panel(whitened, panel_owner[panel], panel_start[panel]))
    sources = jnp.concatenate(pieces, axis=0)
    groups = lax.axis_size("tm")
    inverse = inverse_table(length, 1.0 / math.sqrt(bins * windows_here * segments * groups))
    source_count = sources.shape[0]
    own_rows = whitened.reshape(channels, windows_here * segments, 2 * bins)
    source_rows = sources.reshape(source_count, windows_here * segments, 2 * bins)
    stacked = lax.psum_scatter(
        correlate(source_rows, own_rows), "tm", scatter_dimension=0, tiled=True
    )
    return jnp.dot(stacked, inverse, precision=lax.Precision.HIGHEST)


def edge_first(values, groups):
    return lax.ppermute(values, "tm", [(0, 1), (groups - 1, groups - 2)])


def whiten_kernel(rows_ref, forward_ref, mask_ref, out_ref):
    spectrum = jnp.dot(rows_ref[...], forward_ref[...], preferred_element_type=jnp.float32)
    energy = jnp.mean(spectrum * spectrum, axis=1, keepdims=True)
    scaled = spectrum * lax.rsqrt(energy + 1e-06) * mask_ref[...]
    out_ref[...] = scaled.astype(jnp.bfloat16).reshape(out_ref.shape)


def whiten_segments(rows, mask, forward, chunks):
    segments, channels, length = rows.shape
    width = channels // chunks
    return pl.pallas_call(
        whiten_kernel,
        grid=(segments,),
        in_specs=[
            pl.BlockSpec((None, channels, length), lambda m: (m, 0, 0)),
            pl.BlockSpec((length, length), lambda m: (0, 0)),
            pl.BlockSpec((None, channels, 1), lambda m: (m, 0, 0)),
        ],
        out_specs=pl.BlockSpec((chunks, None, width, length), lambda m: (0, m, 0, 0)),
        out_shape=jax.ShapeDtypeStruct((chunks, segments, width, length), jnp.bfloat16),
    )(rows, forward, mask)


LANES = 128
ROWS = 8


def cross_kernel(own_ref, src_ref, out_ref):
    segments = own_ref.shape[0]
    sources = src_ref.shape[1]
    rows = own_ref.shape[1]
    bins = own_ref.shape[-1] // 2

    def tile_body(tile, carry):
        re_lanes = pl.ds(pl.multiple_of(tile * LANES, LANES), LANES)
        im_lanes = pl.ds(pl.multiple_of(bins + tile * LANES, LANES), LANES)

        def step(m, acc):
            wr = own_ref[m, :, re_lanes].astype(jnp.float32)
            wi = own_ref[m, :, im_lanes].astype(jnp.float32)
            out = []
            for j in range(sources):
                sr = jnp.concatenate([src_ref[m, j, :, re_lanes]] * (rows // ROWS), axis=0)
                si = jnp.concatenate([src_ref[m, j, :, im_lanes]] * (rows // ROWS), axis=0)
                out.append(acc[2 * j] + (wr * sr + wi * si))
                out.append(acc[2 * j + 1] + (wi * sr - wr * si))
            return tuple(out)

        acc = tuple(jnp.zeros((rows, LANES), jnp.float32) for _ in range(2 * sources))
        acc = lax.fori_loop(0, segments, step, acc)
        for j in range(sources):
            out_ref[j, :, re_lanes] = acc[2 * j]
            out_ref[j, :, im_lanes] = acc[2 * j + 1]
        return carry

    lax.fori_loop(0, bins // LANES, tile_body, 0)


def cross_chunk(own, src):
    segments, width, length = own.shape
    sources = src.shape[1]
    step_rows = 2 * ROWS
    return pl.pallas_call(
        cross_kernel,
        grid=(width // step_rows,),
        in_specs=[
            pl.BlockSpec((segments, step_rows, length), lambda i: (0, i, 0)),
            pl.BlockSpec((segments, sources, ROWS, length), lambda i: (0, 0, 0, 0)),
        ],
        out_specs=pl.BlockSpec((sources, step_rows, length), lambda i: (0, i, 0)),
        out_shape=jax.ShapeDtypeStruct((sources, width, length), jnp.float32),
    )(own, src)


def butterfly_sum(values, axis):
    count = lax.axis_size(axis)
    step = 1
    while step < count:
        values = values + lax.ppermute(values, axis, [(b, b ^ step) for b in range(count)])
        step *= 2
    return values


def widen(values, length):
    segments, count = values.shape[0], values.shape[1]
    return jnp.broadcast_to(values.astype(jnp.float32)[:, :, None, :], (segments, count, ROWS, length))


def on_line(traces, valid, panel_owner, panel_start):
    channels, windows_here, segments, length = traces.shape
    bins = length // 2
    groups = lax.axis_size("tm")
    place = lax.axis_index("tm")
    chunks = 8
    width = channels // chunks
    seg_count = windows_here * segments
    sample = jnp.arange(length, dtype=jnp.int32)
    bin_index = jnp.arange(bins, dtype=jnp.int32)
    angles = (sample[:, None] * bin_index[None, :] % length).astype(jnp.float32) * (2.0 * math.pi / length)
    cosine = jnp.cos(angles)
    sine = jnp.sin(angles)
    forward = jnp.concatenate([cosine, -sine], axis=1).astype(jnp.bfloat16)
    rows = traces.reshape(channels, seg_count, length).transpose(1, 0, 2)
    mask = valid.reshape(channels, seg_count).transpose(1, 0).astype(jnp.float32)[:, :, None]
    whitened = whiten_segments(rows, mask, forward, chunks)
    block_place = lax.axis_index("block")
    pieces = []
    for panel in range(NP):
        first = panel_start[panel]
        chunk_of = first // width
        candidate = lax.dynamic_slice_in_dim(
            lax.dynamic_index_in_dim(whitened, chunk_of, 0, keepdims=False), first - chunk_of * width, PP, 1
        )
        pieces.append(jnp.where(block_place == panel_owner[panel], candidate, 0).astype(candidate.dtype))
    sources = butterfly_sum(jnp.concatenate(pieces, axis=1), "block")
    source_count = sources.shape[1]
    per_group = source_count // groups
    half = source_count // 2
    first_half = place < groups // 2
    turned = jnp.concatenate(
        [sources[:, source_count - per_group:], sources[:, half:source_count - per_group]], axis=1
    )
    far = jnp.where(first_half, turned, sources[:, :half])
    near = jnp.where(first_half, sources[:, :half], turned)
    factor = 1.0 / math.sqrt(bins * seg_count * groups)
    weight = jnp.where(bin_index == 0, 1.0, 2.0).astype(jnp.float32)[:, None] * factor
    inverse = jnp.concatenate([weight * cosine.T, -weight * sine.T], axis=0)
    is_edge = jnp.logical_or(place == 0, place == groups - 1)
    far_wide, near_wide = widen(far, length), widen(near, length)
    outs = []
    arrived = []
    for chunk in range(chunks):
        own = whitened[chunk]
        if chunk >= 2:
            own, _ = lax.optimization_barrier((own, arrived[chunk - 2]))
        far_part = cross_chunk(own, far_wide)
        near_part = cross_chunk(own, near_wide)
        edge_out = jnp.concatenate([far_part, near_part[per_group:]], axis=0).astype(jnp.bfloat16)
        if arrived:
            edge_out, _ = lax.optimization_barrier((edge_out, arrived[-1]))
        edge_in = edge_first(edge_out, groups)
        arrived.append(edge_in)
        far_total = far_part + edge_in[:half].astype(jnp.float32)
        got = lax.ppermute(far_total.astype(jnp.bfloat16), "tm", [(1, 2), (2, 1)]).astype(jnp.float32)
        low = near_part[:per_group] + got[:per_group]
        high = near_part[per_group:] + edge_in[half:].astype(jnp.float32) + got[per_group:]
        back = lax.ppermute(low, "tm", [(1, 0), (2, 3)])
        final = jnp.where(is_edge, near_part[:per_group] + back, high)
        outs.append(jnp.dot(final, inverse, precision=lax.Precision.HIGH))
    return jnp.concatenate(outs, axis=1)


def solution(mesh):
    in_specs = (P("block", "tm", None, None), P("block", "tm", None), P(), P())
    out_specs = P("tm", "block", None)
    body = on_line if mesh.shape["tm"] == 4 else on_device
    return jax.shard_map(
        body, mesh=mesh, in_specs=in_specs, out_specs=out_specs, check_vma=False
    )
```

```python
import math

import jax
import jax.numpy as jnp
from jax import lax
from jax.sharding import PartitionSpec as P
from jax.experimental import pallas as pl
from jax.experimental.pallas import tpu as pltpu

PP = 4
NP = 4


def spread(value, axis, source):
    kept = jnp.where(lax.axis_index(axis) == source, value, 0).astype(value.dtype)
    return lax.psum(kept, axis)


def forward_table(length):
    sample = jnp.arange(length, dtype=jnp.int32)
    bin_index = jnp.arange(length // 2, dtype=jnp.int32)
    angles = (sample[:, None] * bin_index[None, :] % length).astype(jnp.float32) * (
        2.0 * math.pi / length
    )
    return jnp.concatenate([jnp.cos(angles), -jnp.sin(angles)], axis=1).astype(jnp.bfloat16)


def inverse_table(length, factor):
    bin_index = jnp.arange(length // 2, dtype=jnp.int32)
    lag_index = jnp.arange(length, dtype=jnp.int32)
    angles = (bin_index[:, None] * lag_index[None, :] % length).astype(jnp.float32) * (
        2.0 * math.pi / length
    )
    weight = jnp.where(bin_index == 0, 1.0, 2.0).astype(jnp.float32)[:, None] * factor
    return jnp.concatenate([weight * jnp.cos(angles), -weight * jnp.sin(angles)], axis=0)


def whiten(segment_rows, valid_mask, forward):
    spectrum = jnp.dot(segment_rows, forward, preferred_element_type=jnp.float32)
    energy = jnp.mean(spectrum * spectrum, axis=1, keepdims=True)
    return (spectrum * lax.rsqrt(energy + 1e-06) * valid_mask[:, None].astype(jnp.float32)).astype(
        jnp.bfloat16
    )


def spectra_rows(segment_rows, valid_mask, forward):
    return whiten(segment_rows, valid_mask, forward)


def correlate(left, right):
    bins = left.shape[-1] // 2
    left_both = jnp.concatenate([left[..., :bins], left[..., bins:]], axis=1)
    right_both = jnp.concatenate([right[..., :bins], right[..., bins:]], axis=1)
    right_turn = jnp.concatenate([right[..., bins:], -right[..., :bins]], axis=1)
    real_part = jnp.einsum(
        "jmk,imk->jik", left_both, right_both, preferred_element_type=jnp.float32
    )
    imag_part = jnp.einsum(
        "jmk,imk->jik", left_both, right_turn, preferred_element_type=jnp.float32
    )
    return jnp.concatenate([real_part, imag_part], axis=-1)


def fetch_panel(whitened, panel_root, panel_first):
    candidate = lax.dynamic_slice_in_dim(whitened, panel_first, PP, 0)
    return spread(candidate, "block", panel_root)


def on_device(traces, valid, panel_owner, panel_start):
    channels, windows_here, segments, length = traces.shape
    bins = length // 2
    forward = forward_table(length)
    whitened = spectra_rows(
        traces.reshape(channels * windows_here * segments, length),
        valid.reshape(channels * windows_here * segments),
        forward,
    )
    whitened = whitened.reshape(channels, windows_here, segments, 2 * bins)
    pieces = []
    for panel in range(NP):
        pieces.append(fetch_panel(whitened, panel_owner[panel], panel_start[panel]))
    sources = jnp.concatenate(pieces, axis=0)
    groups = lax.axis_size("tm")
    inverse = inverse_table(length, 1.0 / math.sqrt(bins * windows_here * segments * groups))
    source_count = sources.shape[0]
    own_rows = whitened.reshape(channels, windows_here * segments, 2 * bins)
    source_rows = sources.reshape(source_count, windows_here * segments, 2 * bins)
    stacked = lax.psum_scatter(
        correlate(source_rows, own_rows), "tm", scatter_dimension=0, tiled=True
    )
    return jnp.dot(stacked, inverse, precision=lax.Precision.HIGHEST)


def edge_first(values, groups):
    return lax.ppermute(values, "tm", [(0, 1), (groups - 1, groups - 2)])


def whiten_kernel(rows_ref, forward_ref, mask_ref, out_ref):
    spectrum = jnp.dot(rows_ref[...], forward_ref[...], preferred_element_type=jnp.float32)
    energy = jnp.mean(spectrum * spectrum, axis=1, keepdims=True)
    scaled = spectrum * lax.rsqrt(energy + 1e-06) * mask_ref[...]
    out_ref[...] = scaled.astype(jnp.bfloat16).reshape(out_ref.shape)


def whiten_segments(rows, mask, forward, chunks):
    segments, channels, length = rows.shape
    width = channels // chunks
    return pl.pallas_call(
        whiten_kernel,
        grid=(segments,),
        in_specs=[
            pl.BlockSpec((None, channels, length), lambda m: (m, 0, 0)),
            pl.BlockSpec((length, length), lambda m: (0, 0)),
            pl.BlockSpec((None, channels, 1), lambda m: (m, 0, 0)),
        ],
        out_specs=pl.BlockSpec((chunks, None, width, length), lambda m: (0, m, 0, 0)),
        out_shape=jax.ShapeDtypeStruct((chunks, segments, width, length), jnp.bfloat16),
    )(rows, forward, mask)


LANES = 128
ROWS = 8


def cross_kernel(own_ref, src_ref, out_ref):
    segments = own_ref.shape[0]
    sources = src_ref.shape[1]
    bins = own_ref.shape[-1] // 2

    def tile_body(index, carry):
        half = index // (bins // LANES)
        tile = index % (bins // LANES)
        rows = pl.ds(pl.multiple_of(half * ROWS, ROWS), ROWS)
        re_lanes = pl.ds(pl.multiple_of(tile * LANES, LANES), LANES)
        im_lanes = pl.ds(pl.multiple_of(bins + tile * LANES, LANES), LANES)

        def step(m, acc):
            wr = own_ref[m, rows, re_lanes].astype(jnp.float32)
            wi = own_ref[m, rows, im_lanes].astype(jnp.float32)
            out = []
            for j in range(sources):
                sr = src_ref[m, j, :, re_lanes]
                si = src_ref[m, j, :, im_lanes]
                out.append(acc[2 * j] + (wr * sr + wi * si))
                out.append(acc[2 * j + 1] + (wi * sr - wr * si))
            return tuple(out)

        acc = tuple(jnp.zeros((ROWS, LANES), jnp.float32) for _ in range(2 * sources))
        acc = lax.fori_loop(0, segments, step, acc)
        for j in range(sources):
            out_ref[j, rows, re_lanes] = acc[2 * j]
            out_ref[j, rows, im_lanes] = acc[2 * j + 1]
        return carry

    lax.fori_loop(0, (own_ref.shape[1] // ROWS) * (bins // LANES), tile_body, 0)


def cross_chunk(own, src):
    segments, width, length = own.shape
    sources = src.shape[1]
    step_rows = 2 * ROWS
    return pl.pallas_call(
        cross_kernel,
        grid=(width // step_rows,),
        in_specs=[
            pl.BlockSpec((segments, step_rows, length), lambda i: (0, i, 0)),
            pl.BlockSpec((segments, sources, ROWS, length), lambda i: (0, 0, 0, 0)),
        ],
        out_specs=pl.BlockSpec((sources, step_rows, length), lambda i: (0, i, 0)),
        out_shape=jax.ShapeDtypeStruct((sources, width, length), jnp.float32),
    )(own, src)


def butterfly_sum(values, axis):
    count = lax.axis_size(axis)
    step = 1
    while step < count:
        values = values + lax.ppermute(values, axis, [(b, b ^ step) for b in range(count)])
        step *= 2
    return values


def widen(values, length):
    segments, count = values.shape[0], values.shape[1]
    return jnp.broadcast_to(values.astype(jnp.float32)[:, :, None, :], (segments, count, ROWS, length))


def on_line(traces, valid, panel_owner, panel_start):
    channels, windows_here, segments, length = traces.shape
    bins = length // 2
    groups = lax.axis_size("tm")
    place = lax.axis_index("tm")
    chunks = 8
    width = channels // chunks
    seg_count = windows_here * segments
    sample = jnp.arange(length, dtype=jnp.int32)
    bin_index = jnp.arange(bins, dtype=jnp.int32)
    angles = (sample[:, None] * bin_index[None, :] % length).astype(jnp.float32) * (2.0 * math.pi / length)
    cosine, sine = lax.optimization_barrier((jnp.cos(angles), jnp.sin(angles)))
    forward = jnp.concatenate([cosine, -sine], axis=1).astype(jnp.bfloat16)
    rows = traces.reshape(channels, seg_count, length).transpose(1, 0, 2)
    mask = valid.reshape(channels, seg_count).transpose(1, 0).astype(jnp.float32)[:, :, None]
    whitened = whiten_segments(rows, mask, forward, chunks)
    block_place = lax.axis_index("block")
    pieces = []
    for panel in range(NP):
        first = panel_start[panel]
        chunk_of = first // width
        candidate = lax.dynamic_slice_in_dim(
            lax.dynamic_index_in_dim(whitened, chunk_of, 0, keepdims=False), first - chunk_of * width, PP, 1
        )
        pieces.append(jnp.where(block_place == panel_owner[panel], candidate, 0).astype(candidate.dtype))
    sources = butterfly_sum(jnp.concatenate(pieces, axis=1), "block")
    source_count = sources.shape[1]
    per_group = source_count // groups
    half = source_count // 2
    first_half = place < groups // 2
    turned = jnp.concatenate(
        [sources[:, source_count - per_group:], sources[:, half:source_count - per_group]], axis=1
    )
    far = jnp.where(first_half, turned, sources[:, :half])
    near = jnp.where(first_half, sources[:, :half], turned)
    factor = 1.0 / math.sqrt(bins * seg_count * groups)
    weight = jnp.where(bin_index == 0, 1.0, 2.0).astype(jnp.float32)[:, None] * factor
    inverse = jnp.concatenate([weight * cosine.T, -weight * sine.T], axis=0)
    is_edge = jnp.logical_or(place == 0, place == groups - 1)
    order = jnp.concatenate([far, near[:, per_group:], near[:, :per_group]], axis=1)
    order_wide = widen(order, length)
    outs = []
    arrived = []
    for chunk in range(chunks):
        own = whitened[chunk]
        if chunk >= 2:
            own, _ = lax.optimization_barrier((own, arrived[chunk - 2]))
        part = cross_chunk(own, order_wide)
        far_part = part[:half]
        near_part = jnp.concatenate([part[source_count - per_group:], part[half:source_count - per_group]], axis=0)
        edge_out = part[:source_count - per_group].astype(jnp.bfloat16)
        if arrived:
            edge_out, _ = lax.optimization_barrier((edge_out, arrived[-1]))
        edge_in = edge_first(edge_out, groups)
        arrived.append(edge_in)
        far_total = far_part + edge_in[:half].astype(jnp.float32)
        got = lax.ppermute(far_total.astype(jnp.bfloat16), "tm", [(1, 2), (2, 1)]).astype(jnp.float32)
        low = near_part[:per_group] + got[:per_group]
        high = near_part[per_group:] + edge_in[half:].astype(jnp.float32) + got[per_group:]
        back = lax.ppermute(low, "tm", [(1, 0), (2, 3)])
        final = jnp.where(is_edge, near_part[:per_group] + back, high)
        outs.append(jnp.dot(final, inverse, precision=lax.Precision.HIGH))
    return jnp.concatenate(outs, axis=1)


def solution(mesh):
    in_specs = (P("block", "tm", None, None), P("block", "tm", None), P(), P())
    out_specs = P("tm", "block", None)
    body = on_line if mesh.shape["tm"] == 4 else on_device
    return jax.shard_map(
        body, mesh=mesh, in_specs=in_specs, out_specs=out_specs, check_vma=False
    )
```

```python
import math

import jax
import jax.numpy as jnp
from jax import lax
from jax.sharding import PartitionSpec as P
from jax.experimental import pallas as pl
from jax.experimental.pallas import tpu as pltpu

PP = 4
NP = 4


def spread(value, axis, source):
    kept = jnp.where(lax.axis_index(axis) == source, value, 0).astype(value.dtype)
    return lax.psum(kept, axis)


def forward_table(length):
    sample = jnp.arange(length, dtype=jnp.int32)
    bin_index = jnp.arange(length // 2, dtype=jnp.int32)
    angles = (sample[:, None] * bin_index[None, :] % length).astype(jnp.float32) * (
        2.0 * math.pi / length
    )
    return jnp.concatenate([jnp.cos(angles), -jnp.sin(angles)], axis=1).astype(jnp.bfloat16)


def inverse_table(length, factor):
    bin_index = jnp.arange(length // 2, dtype=jnp.int32)
    lag_index = jnp.arange(length, dtype=jnp.int32)
    angles = (bin_index[:, None] * lag_index[None, :] % length).astype(jnp.float32) * (
        2.0 * math.pi / length
    )
    weight = jnp.where(bin_index == 0, 1.0, 2.0).astype(jnp.float32)[:, None] * factor
    return jnp.concatenate([weight * jnp.cos(angles), -weight * jnp.sin(angles)], axis=0)


def whiten(segment_rows, valid_mask, forward):
    spectrum = jnp.dot(segment_rows, forward, preferred_element_type=jnp.float32)
    energy = jnp.mean(spectrum * spectrum, axis=1, keepdims=True)
    return (spectrum * lax.rsqrt(energy + 1e-06) * valid_mask[:, None].astype(jnp.float32)).astype(
        jnp.bfloat16
    )


def spectra_rows(segment_rows, valid_mask, forward):
    return whiten(segment_rows, valid_mask, forward)


def correlate(left, right):
    bins = left.shape[-1] // 2
    left_both = jnp.concatenate([left[..., :bins], left[..., bins:]], axis=1)
    right_both = jnp.concatenate([right[..., :bins], right[..., bins:]], axis=1)
    right_turn = jnp.concatenate([right[..., bins:], -right[..., :bins]], axis=1)
    real_part = jnp.einsum(
        "jmk,imk->jik", left_both, right_both, preferred_element_type=jnp.float32
    )
    imag_part = jnp.einsum(
        "jmk,imk->jik", left_both, right_turn, preferred_element_type=jnp.float32
    )
    return jnp.concatenate([real_part, imag_part], axis=-1)


def fetch_panel(whitened, panel_root, panel_first):
    candidate = lax.dynamic_slice_in_dim(whitened, panel_first, PP, 0)
    return spread(candidate, "block", panel_root)


def on_device(traces, valid, panel_owner, panel_start):
    channels, windows_here, segments, length = traces.shape
    bins = length // 2
    forward = forward_table(length)
    whitened = spectra_rows(
        traces.reshape(channels * windows_here * segments, length),
        valid.reshape(channels * windows_here * segments),
        forward,
    )
    whitened = whitened.reshape(channels, windows_here, segments, 2 * bins)
    pieces = []
    for panel in range(NP):
        pieces.append(fetch_panel(whitened, panel_owner[panel], panel_start[panel]))
    sources = jnp.concatenate(pieces, axis=0)
    groups = lax.axis_size("tm")
    inverse = inverse_table(length, 1.0 / math.sqrt(bins * windows_here * segments * groups))
    source_count = sources.shape[0]
    own_rows = whitened.reshape(channels, windows_here * segments, 2 * bins)
    source_rows = sources.reshape(source_count, windows_here * segments, 2 * bins)
    stacked = lax.psum_scatter(
        correlate(source_rows, own_rows), "tm", scatter_dimension=0, tiled=True
    )
    return jnp.dot(stacked, inverse, precision=lax.Precision.HIGHEST)


def edge_first(values, groups):
    return lax.ppermute(values, "tm", [(0, 1), (groups - 1, groups - 2)])


def whiten_kernel(rows_ref, forward_ref, mask_ref, out_ref):
    spectrum = jnp.dot(rows_ref[...], forward_ref[...], preferred_element_type=jnp.float32)
    energy = jnp.mean(spectrum * spectrum, axis=1, keepdims=True)
    scaled = spectrum * lax.rsqrt(energy + 1e-06) * mask_ref[...]
    out_ref[...] = scaled.astype(jnp.bfloat16).reshape(out_ref.shape)


def whiten_segments(rows, mask, forward, chunks):
    segments, channels, length = rows.shape
    width = channels // chunks
    return pl.pallas_call(
        whiten_kernel,
        grid=(segments,),
        in_specs=[
            pl.BlockSpec((None, channels, length), lambda m: (m, 0, 0)),
            pl.BlockSpec((length, length), lambda m: (0, 0)),
            pl.BlockSpec((None, channels, 1), lambda m: (m, 0, 0)),
        ],
        out_specs=pl.BlockSpec((chunks, None, width, length), lambda m: (0, m, 0, 0)),
        out_shape=jax.ShapeDtypeStruct((chunks, segments, width, length), jnp.bfloat16),
    )(rows, forward, mask)


LANES = 128
ROWS = 8


def cross_kernel(own_ref, src_ref, out_ref):
    segments = own_ref.shape[0]
    sources = src_ref.shape[1]
    bins = own_ref.shape[-1] // 2

    def tile_body(index, carry):
        half = index // (bins // LANES)
        tile = index % (bins // LANES)
        rows = pl.ds(pl.multiple_of(half * ROWS, ROWS), ROWS)
        re_lanes = pl.ds(pl.multiple_of(tile * LANES, LANES), LANES)
        im_lanes = pl.ds(pl.multiple_of(bins + tile * LANES, LANES), LANES)

        def step(m, acc):
            wr = own_ref[m, rows, re_lanes].astype(jnp.float32)
            wi = own_ref[m, rows, im_lanes].astype(jnp.float32)
            out = []
            for j in range(sources):
                sr = src_ref[m, j, :, re_lanes]
                si = src_ref[m, j, :, im_lanes]
                out.append(acc[2 * j] + (wr * sr + wi * si))
                out.append(acc[2 * j + 1] + (wi * sr - wr * si))
            return tuple(out)

        acc = tuple(jnp.zeros((ROWS, LANES), jnp.float32) for _ in range(2 * sources))
        acc = lax.fori_loop(0, segments, step, acc)
        for j in range(sources):
            out_ref[j, rows, re_lanes] = acc[2 * j]
            out_ref[j, rows, im_lanes] = acc[2 * j + 1]
        return carry

    lax.fori_loop(0, (own_ref.shape[1] // ROWS) * (bins // LANES), tile_body, 0)


def cross_chunk(own, src):
    segments, width, length = own.shape
    sources = src.shape[1]
    step_rows = 2 * ROWS
    return pl.pallas_call(
        cross_kernel,
        grid=(width // step_rows,),
        in_specs=[
            pl.BlockSpec((segments, step_rows, length), lambda i: (0, i, 0)),
            pl.BlockSpec((segments, sources, ROWS, length), lambda i: (0, 0, 0, 0)),
        ],
        out_specs=pl.BlockSpec((sources, step_rows, length), lambda i: (0, i, 0)),
        out_shape=jax.ShapeDtypeStruct((sources, width, length), jnp.float32),
    )(own, src)


def butterfly_sum(values, axis):
    count = lax.axis_size(axis)
    step = 1
    while step < count:
        values = values + lax.ppermute(values, axis, [(b, b ^ step) for b in range(count)])
        step *= 2
    return values


def widen(values, length):
    segments, count = values.shape[0], values.shape[1]
    return jnp.broadcast_to(values.astype(jnp.float32)[:, :, None, :], (segments, count, ROWS, length))


def on_line(traces, valid, panel_owner, panel_start):
    channels, windows_here, segments, length = traces.shape
    bins = length // 2
    groups = lax.axis_size("tm")
    place = lax.axis_index("tm")
    chunks = 4
    width = channels // chunks
    seg_count = windows_here * segments
    sample = jnp.arange(length, dtype=jnp.int32)
    bin_index = jnp.arange(bins, dtype=jnp.int32)
    angles = (sample[:, None] * bin_index[None, :] % length).astype(jnp.float32) * (2.0 * math.pi / length)
    cosine, sine = lax.optimization_barrier((jnp.cos(angles), jnp.sin(angles)))
    forward = jnp.concatenate([cosine, -sine], axis=1).astype(jnp.bfloat16)
    rows = traces.reshape(channels, seg_count, length).transpose(1, 0, 2)
    mask = valid.reshape(channels, seg_count).transpose(1, 0).astype(jnp.float32)[:, :, None]
    whitened = whiten_segments(rows, mask, forward, chunks)
    block_place = lax.axis_index("block")
    pieces = []
    for panel in range(NP):
        first = panel_start[panel]
        chunk_of = first // width
        candidate = lax.dynamic_slice_in_dim(
            lax.dynamic_index_in_dim(whitened, chunk_of, 0, keepdims=False), first - chunk_of * width, PP, 1
        )
        pieces.append(jnp.where(block_place == panel_owner[panel], candidate, 0).astype(candidate.dtype))
    sources = butterfly_sum(jnp.concatenate(pieces, axis=1), "block")
    source_count = sources.shape[1]
    per_group = source_count // groups
    half = source_count // 2
    first_half = place < groups // 2
    turned = jnp.concatenate(
        [sources[:, source_count - per_group:], sources[:, half:source_count - per_group]], axis=1
    )
    far = jnp.where(first_half, turned, sources[:, :half])
    near = jnp.where(first_half, sources[:, :half], turned)
    factor = 1.0 / math.sqrt(bins * seg_count * groups)
    weight = jnp.where(bin_index == 0, 1.0, 2.0).astype(jnp.float32)[:, None] * factor
    inverse = jnp.concatenate([weight * cosine.T, -weight * sine.T], axis=0)
    is_edge = jnp.logical_or(place == 0, place == groups - 1)
    order = jnp.concatenate([far, near[:, per_group:], near[:, :per_group]], axis=1)
    order_wide = widen(order, length)
    outs = []
    arrived = []
    for chunk in range(chunks):
        own = whitened[chunk]
        if chunk >= 2:
            own, _ = lax.optimization_barrier((own, arrived[chunk - 2]))
        part = cross_chunk(own, order_wide)
        far_part = part[:half]
        near_part = jnp.concatenate([part[source_count - per_group:], part[half:source_count - per_group]], axis=0)
        edge_out = part[:source_count - per_group].astype(jnp.bfloat16)
        if arrived:
            edge_out, _ = lax.optimization_barrier((edge_out, arrived[-1]))
        edge_in = edge_first(edge_out, groups)
        arrived.append(edge_in)
        far_total = far_part + edge_in[:half].astype(jnp.float32)
        got = lax.ppermute(far_total.astype(jnp.bfloat16), "tm", [(1, 2), (2, 1)]).astype(jnp.float32)
        low = near_part[:per_group] + got[:per_group]
        high = near_part[per_group:] + edge_in[half:].astype(jnp.float32) + got[per_group:]
        back = lax.ppermute(low, "tm", [(1, 0), (2, 3)])
        final = jnp.where(is_edge, near_part[:per_group] + back, high)
        outs.append(jnp.dot(final, inverse, precision=lax.Precision.HIGH))
    return jnp.concatenate(outs, axis=1)


def solution(mesh):
    in_specs = (P("block", "tm", None, None), P("block", "tm", None), P(), P())
    out_specs = P("tm", "block", None)
    body = on_line if mesh.shape["tm"] == 4 else on_device
    return jax.shard_map(
        body, mesh=mesh, in_specs=in_specs, out_specs=out_specs, check_vma=False
    )
```

```python
import math

import jax
import jax.numpy as jnp
from jax import lax
from jax.sharding import PartitionSpec as P
from jax.experimental import pallas as pl
from jax.experimental.pallas import tpu as pltpu

PP = 4
NP = 4


def spread(value, axis, source):
    kept = jnp.where(lax.axis_index(axis) == source, value, 0).astype(value.dtype)
    return lax.psum(kept, axis)


def forward_table(length):
    sample = jnp.arange(length, dtype=jnp.int32)
    bin_index = jnp.arange(length // 2, dtype=jnp.int32)
    angles = (sample[:, None] * bin_index[None, :] % length).astype(jnp.float32) * (
        2.0 * math.pi / length
    )
    return jnp.concatenate([jnp.cos(angles), -jnp.sin(angles)], axis=1).astype(jnp.bfloat16)


def inverse_table(length, factor):
    bin_index = jnp.arange(length // 2, dtype=jnp.int32)
    lag_index = jnp.arange(length, dtype=jnp.int32)
    angles = (bin_index[:, None] * lag_index[None, :] % length).astype(jnp.float32) * (
        2.0 * math.pi / length
    )
    weight = jnp.where(bin_index == 0, 1.0, 2.0).astype(jnp.float32)[:, None] * factor
    return jnp.concatenate([weight * jnp.cos(angles), -weight * jnp.sin(angles)], axis=0)


def whiten(segment_rows, valid_mask, forward):
    spectrum = jnp.dot(segment_rows, forward, preferred_element_type=jnp.float32)
    energy = jnp.mean(spectrum * spectrum, axis=1, keepdims=True)
    return (spectrum * lax.rsqrt(energy + 1e-06) * valid_mask[:, None].astype(jnp.float32)).astype(
        jnp.bfloat16
    )


def spectra_rows(segment_rows, valid_mask, forward):
    return whiten(segment_rows, valid_mask, forward)


def correlate(left, right):
    bins = left.shape[-1] // 2
    left_both = jnp.concatenate([left[..., :bins], left[..., bins:]], axis=1)
    right_both = jnp.concatenate([right[..., :bins], right[..., bins:]], axis=1)
    right_turn = jnp.concatenate([right[..., bins:], -right[..., :bins]], axis=1)
    real_part = jnp.einsum(
        "jmk,imk->jik", left_both, right_both, preferred_element_type=jnp.float32
    )
    imag_part = jnp.einsum(
        "jmk,imk->jik", left_both, right_turn, preferred_element_type=jnp.float32
    )
    return jnp.concatenate([real_part, imag_part], axis=-1)


def fetch_panel(whitened, panel_root, panel_first):
    candidate = lax.dynamic_slice_in_dim(whitened, panel_first, PP, 0)
    return spread(candidate, "block", panel_root)


def on_device(traces, valid, panel_owner, panel_start):
    channels, windows_here, segments, length = traces.shape
    bins = length // 2
    forward = forward_table(length)
    whitened = spectra_rows(
        traces.reshape(channels * windows_here * segments, length),
        valid.reshape(channels * windows_here * segments),
        forward,
    )
    whitened = whitened.reshape(channels, windows_here, segments, 2 * bins)
    pieces = []
    for panel in range(NP):
        pieces.append(fetch_panel(whitened, panel_owner[panel], panel_start[panel]))
    sources = jnp.concatenate(pieces, axis=0)
    groups = lax.axis_size("tm")
    inverse = inverse_table(length, 1.0 / math.sqrt(bins * windows_here * segments * groups))
    source_count = sources.shape[0]
    own_rows = whitened.reshape(channels, windows_here * segments, 2 * bins)
    source_rows = sources.reshape(source_count, windows_here * segments, 2 * bins)
    stacked = lax.psum_scatter(
        correlate(source_rows, own_rows), "tm", scatter_dimension=0, tiled=True
    )
    return jnp.dot(stacked, inverse, precision=lax.Precision.HIGHEST)


def edge_first(values, groups):
    return lax.ppermute(values, "tm", [(0, 1), (groups - 1, groups - 2)])


def whiten_kernel(rows_ref, forward_ref, mask_ref, out_ref):
    spectrum = jnp.dot(rows_ref[...], forward_ref[...], preferred_element_type=jnp.float32)
    energy = jnp.mean(spectrum * spectrum, axis=1, keepdims=True)
    scaled = spectrum * lax.rsqrt(energy + 1e-06) * mask_ref[...]
    out_ref[...] = scaled.astype(jnp.bfloat16).reshape(out_ref.shape)


def whiten_segments(rows, mask, forward, chunks):
    segments, channels, length = rows.shape
    width = channels // chunks
    return pl.pallas_call(
        whiten_kernel,
        grid=(segments,),
        in_specs=[
            pl.BlockSpec((None, channels, length), lambda m: (m, 0, 0)),
            pl.BlockSpec((length, length), lambda m: (0, 0)),
            pl.BlockSpec((None, channels, 1), lambda m: (m, 0, 0)),
        ],
        out_specs=pl.BlockSpec((chunks, None, width, length), lambda m: (0, m, 0, 0)),
        out_shape=jax.ShapeDtypeStruct((chunks, segments, width, length), jnp.bfloat16),
    )(rows, forward, mask)


LANES = 128
ROWS = 8


def cross_kernel(own_ref, src_ref, out_ref):
    segments = own_ref.shape[0]
    sources = src_ref.shape[1]
    bins = own_ref.shape[-1] // 2

    def tile_body(index, carry):
        half = index // (bins // LANES)
        tile = index % (bins // LANES)
        rows = pl.ds(pl.multiple_of(half * ROWS, ROWS), ROWS)
        re_lanes = pl.ds(pl.multiple_of(tile * LANES, LANES), LANES)
        im_lanes = pl.ds(pl.multiple_of(bins + tile * LANES, LANES), LANES)

        def step(m, acc):
            wr = own_ref[m, rows, re_lanes].astype(jnp.float32)
            wi = own_ref[m, rows, im_lanes].astype(jnp.float32)
            out = []
            for j in range(sources):
                sr = src_ref[m, j, :, re_lanes]
                si = src_ref[m, j, :, im_lanes]
                out.append(acc[2 * j] + (wr * sr + wi * si))
                out.append(acc[2 * j + 1] + (wi * sr - wr * si))
            return tuple(out)

        acc = tuple(jnp.zeros((ROWS, LANES), jnp.float32) for _ in range(2 * sources))
        acc = lax.fori_loop(0, segments, step, acc)
        for j in range(sources):
            out_ref[j, rows, re_lanes] = acc[2 * j]
            out_ref[j, rows, im_lanes] = acc[2 * j + 1]
        return carry

    lax.fori_loop(0, (own_ref.shape[1] // ROWS) * (bins // LANES), tile_body, 0)


def cross_chunk(own, src):
    segments, width, length = own.shape
    sources = src.shape[1]
    step_rows = 2 * ROWS
    return pl.pallas_call(
        cross_kernel,
        grid=(width // step_rows,),
        in_specs=[
            pl.BlockSpec((segments, step_rows, length), lambda i: (0, i, 0)),
            pl.BlockSpec((segments, sources, ROWS, length), lambda i: (0, 0, 0, 0)),
        ],
        out_specs=pl.BlockSpec((sources, step_rows, length), lambda i: (0, i, 0)),
        out_shape=jax.ShapeDtypeStruct((sources, width, length), jnp.float32),
    )(own, src)


def butterfly_sum(values, axis):
    count = lax.axis_size(axis)
    step = 1
    while step < count:
        values = values + lax.ppermute(values, axis, [(b, b ^ step) for b in range(count)])
        step *= 2
    return values


def widen(values, length):
    segments, count = values.shape[0], values.shape[1]
    return jnp.broadcast_to(values.astype(jnp.float32)[:, :, None, :], (segments, count, ROWS, length))


def on_line(traces, valid, panel_owner, panel_start):
    channels, windows_here, segments, length = traces.shape
    bins = length // 2
    groups = lax.axis_size("tm")
    place = lax.axis_index("tm")
    chunks = 8
    width = channels // chunks
    seg_count = windows_here * segments
    sample = jnp.arange(length, dtype=jnp.int32)
    bin_index = jnp.arange(bins, dtype=jnp.int32)
    angles = (sample[:, None] * bin_index[None, :] % length).astype(jnp.float32) * (2.0 * math.pi / length)
    cosine, sine = lax.optimization_barrier((jnp.cos(angles), jnp.sin(angles)))
    forward = jnp.concatenate([cosine, -sine], axis=1).astype(jnp.bfloat16)
    rows = traces.reshape(channels, seg_count, length).transpose(1, 0, 2)
    mask = valid.reshape(channels, seg_count).transpose(1, 0).astype(jnp.float32)[:, :, None]
    whitened = whiten_segments(rows, mask, forward, chunks)
    block_place = lax.axis_index("block")
    pieces = []
    for panel in range(NP):
        first = panel_start[panel]
        chunk_of = first // width
        candidate = lax.dynamic_slice_in_dim(
            lax.dynamic_index_in_dim(whitened, chunk_of, 0, keepdims=False), first - chunk_of * width, PP, 1
        )
        pieces.append(jnp.where(block_place == panel_owner[panel], candidate, 0).astype(candidate.dtype))
    sources = butterfly_sum(jnp.concatenate(pieces, axis=1), "block")
    source_count = sources.shape[1]
    per_group = source_count // groups
    half = source_count // 2
    first_half = place < groups // 2
    turned = jnp.concatenate(
        [sources[:, source_count - per_group:], sources[:, half:source_count - per_group]], axis=1
    )
    far = jnp.where(first_half, turned, sources[:, :half])
    near = jnp.where(first_half, sources[:, :half], turned)
    factor = 1.0 / math.sqrt(bins * seg_count * groups)
    weight = jnp.where(bin_index == 0, 1.0, 2.0).astype(jnp.float32)[:, None] * factor
    inverse = jnp.concatenate([weight * cosine.T, -weight * sine.T], axis=0)
    is_edge = jnp.logical_or(place == 0, place == groups - 1)
    order = jnp.concatenate([far, near[:, per_group:], near[:, :per_group]], axis=1)
    order_wide = widen(order, length)
    outs = []
    arrived = []
    returned = []
    for chunk in range(chunks):
        own = whitened[chunk]
        if chunk >= 3:
            own, _, _ = lax.optimization_barrier((own, arrived[chunk - 2], returned[chunk - 3]))
        elif chunk >= 2:
            own, _ = lax.optimization_barrier((own, arrived[chunk - 2]))
        part = cross_chunk(own, order_wide)
        far_part = part[:half]
        near_part = jnp.concatenate([part[source_count - per_group:], part[half:source_count - per_group]], axis=0)
        edge_out = part[:source_count - per_group].astype(jnp.bfloat16)
        if arrived:
            edge_out, _ = lax.optimization_barrier((edge_out, arrived[-1]))
        edge_in = edge_first(edge_out, groups)
        arrived.append(edge_in)
        far_total = far_part + edge_in[:half].astype(jnp.float32)
        got = lax.ppermute(far_total.astype(jnp.bfloat16), "tm", [(1, 2), (2, 1)]).astype(jnp.float32)
        low = near_part[:per_group] + got[:per_group]
        high = near_part[per_group:] + edge_in[half:].astype(jnp.float32) + got[per_group:]
        back = lax.ppermute(low, "tm", [(1, 0), (2, 3)])
        returned.append(back)
        final = jnp.where(is_edge, near_part[:per_group] + back, high)
        outs.append(jnp.dot(final, inverse, precision=lax.Precision.HIGH))
    return jnp.concatenate(outs, axis=1)


def solution(mesh):
    in_specs = (P("block", "tm", None, None), P("block", "tm", None), P(), P())
    out_specs = P("tm", "block", None)
    body = on_line if mesh.shape["tm"] == 4 else on_device
    return jax.shard_map(
        body, mesh=mesh, in_specs=in_specs, out_specs=out_specs, check_vma=False
    )
```

```python
import math

import jax
import jax.numpy as jnp
from jax import lax
from jax.sharding import PartitionSpec as P
from jax.experimental import pallas as pl
from jax.experimental.pallas import tpu as pltpu

PP = 4
NP = 4


def spread(value, axis, source):
    kept = jnp.where(lax.axis_index(axis) == source, value, 0).astype(value.dtype)
    return lax.psum(kept, axis)


def forward_table(length):
    sample = jnp.arange(length, dtype=jnp.int32)
    bin_index = jnp.arange(length // 2, dtype=jnp.int32)
    angles = (sample[:, None] * bin_index[None, :] % length).astype(jnp.float32) * (
        2.0 * math.pi / length
    )
    return jnp.concatenate([jnp.cos(angles), -jnp.sin(angles)], axis=1).astype(jnp.bfloat16)


def inverse_table(length, factor):
    bin_index = jnp.arange(length // 2, dtype=jnp.int32)
    lag_index = jnp.arange(length, dtype=jnp.int32)
    angles = (bin_index[:, None] * lag_index[None, :] % length).astype(jnp.float32) * (
        2.0 * math.pi / length
    )
    weight = jnp.where(bin_index == 0, 1.0, 2.0).astype(jnp.float32)[:, None] * factor
    return jnp.concatenate([weight * jnp.cos(angles), -weight * jnp.sin(angles)], axis=0)


def whiten(segment_rows, valid_mask, forward):
    spectrum = jnp.dot(segment_rows, forward, preferred_element_type=jnp.float32)
    energy = jnp.mean(spectrum * spectrum, axis=1, keepdims=True)
    return (spectrum * lax.rsqrt(energy + 1e-06) * valid_mask[:, None].astype(jnp.float32)).astype(
        jnp.bfloat16
    )


def spectra_rows(segment_rows, valid_mask, forward):
    return whiten(segment_rows, valid_mask, forward)


def correlate(left, right):
    bins = left.shape[-1] // 2
    left_both = jnp.concatenate([left[..., :bins], left[..., bins:]], axis=1)
    right_both = jnp.concatenate([right[..., :bins], right[..., bins:]], axis=1)
    right_turn = jnp.concatenate([right[..., bins:], -right[..., :bins]], axis=1)
    real_part = jnp.einsum(
        "jmk,imk->jik", left_both, right_both, preferred_element_type=jnp.float32
    )
    imag_part = jnp.einsum(
        "jmk,imk->jik", left_both, right_turn, preferred_element_type=jnp.float32
    )
    return jnp.concatenate([real_part, imag_part], axis=-1)


def fetch_panel(whitened, panel_root, panel_first):
    candidate = lax.dynamic_slice_in_dim(whitened, panel_first, PP, 0)
    return spread(candidate, "block", panel_root)


def on_device(traces, valid, panel_owner, panel_start):
    channels, windows_here, segments, length = traces.shape
    bins = length // 2
    forward = forward_table(length)
    whitened = spectra_rows(
        traces.reshape(channels * windows_here * segments, length),
        valid.reshape(channels * windows_here * segments),
        forward,
    )
    whitened = whitened.reshape(channels, windows_here, segments, 2 * bins)
    pieces = []
    for panel in range(NP):
        pieces.append(fetch_panel(whitened, panel_owner[panel], panel_start[panel]))
    sources = jnp.concatenate(pieces, axis=0)
    groups = lax.axis_size("tm")
    inverse = inverse_table(length, 1.0 / math.sqrt(bins * windows_here * segments * groups))
    source_count = sources.shape[0]
    own_rows = whitened.reshape(channels, windows_here * segments, 2 * bins)
    source_rows = sources.reshape(source_count, windows_here * segments, 2 * bins)
    stacked = lax.psum_scatter(
        correlate(source_rows, own_rows), "tm", scatter_dimension=0, tiled=True
    )
    return jnp.dot(stacked, inverse, precision=lax.Precision.HIGHEST)


def edge_first(values, groups):
    return lax.ppermute(values, "tm", [(0, 1), (groups - 1, groups - 2)])


def whiten_kernel(rows_ref, forward_ref, mask_ref, out_ref):
    for m in range(rows_ref.shape[1]):
        spectrum = jnp.dot(rows_ref[:, m, :], forward_ref[...], preferred_element_type=jnp.float32)
        energy = jnp.mean(spectrum * spectrum, axis=1, keepdims=True)
        scaled = spectrum * lax.rsqrt(energy + 1e-06) * mask_ref[m]
        out_ref[:, m] = scaled.astype(jnp.bfloat16).reshape(out_ref.shape[0], out_ref.shape[2], out_ref.shape[3])


def whiten_segments(rows, mask, forward, chunks):
    channels, segments, length = rows.shape
    width = channels // chunks
    return pl.pallas_call(
        whiten_kernel,
        grid=(1,),
        in_specs=[
            pl.BlockSpec((channels, segments, length), lambda m: (0, 0, 0)),
            pl.BlockSpec((length, length), lambda m: (0, 0)),
            pl.BlockSpec((segments, channels, 1), lambda m: (0, 0, 0)),
        ],
        out_specs=pl.BlockSpec((chunks, segments, width, length), lambda m: (0, 0, 0, 0)),
        out_shape=jax.ShapeDtypeStruct((chunks, segments, width, length), jnp.bfloat16),
        compiler_params=pltpu.CompilerParams(vmem_limit_bytes=100 * 1024 * 1024),
    )(rows, forward, mask)


LANES = 128
ROWS = 8


def cross_kernel(own_ref, src_ref, out_ref):
    segments = own_ref.shape[0]
    sources = src_ref.shape[1]
    bins = own_ref.shape[-1] // 2

    def tile_body(index, carry):
        half = index // (bins // LANES)
        tile = index % (bins // LANES)
        rows = pl.ds(pl.multiple_of(half * ROWS, ROWS), ROWS)
        re_lanes = pl.ds(pl.multiple_of(tile * LANES, LANES), LANES)
        im_lanes = pl.ds(pl.multiple_of(bins + tile * LANES, LANES), LANES)

        def step(m, acc):
            wr = own_ref[m, rows, re_lanes].astype(jnp.float32)
            wi = own_ref[m, rows, im_lanes].astype(jnp.float32)
            out = []
            for j in range(sources):
                sr = src_ref[m, j, :, re_lanes]
                si = src_ref[m, j, :, im_lanes]
                out.append(acc[2 * j] + (wr * sr + wi * si))
                out.append(acc[2 * j + 1] + (wi * sr - wr * si))
            return tuple(out)

        acc = tuple(jnp.zeros((ROWS, LANES), jnp.float32) for _ in range(2 * sources))
        acc = lax.fori_loop(0, segments, step, acc)
        for j in range(sources):
            out_ref[j, rows, re_lanes] = acc[2 * j]
            out_ref[j, rows, im_lanes] = acc[2 * j + 1]
        return carry

    lax.fori_loop(0, (own_ref.shape[1] // ROWS) * (bins // LANES), tile_body, 0)


def cross_chunk(own, src):
    segments, width, length = own.shape
    sources = src.shape[1]
    step_rows = 2 * ROWS
    return pl.pallas_call(
        cross_kernel,
        grid=(width // step_rows,),
        in_specs=[
            pl.BlockSpec((segments, step_rows, length), lambda i: (0, i, 0)),
            pl.BlockSpec((segments, sources, ROWS, length), lambda i: (0, 0, 0, 0)),
        ],
        out_specs=pl.BlockSpec((sources, step_rows, length), lambda i: (0, i, 0)),
        out_shape=jax.ShapeDtypeStruct((sources, width, length), jnp.float32),
    )(own, src)


def butterfly_sum(values, axis):
    count = lax.axis_size(axis)
    step = 1
    while step < count:
        values = values + lax.ppermute(values, axis, [(b, b ^ step) for b in range(count)])
        step *= 2
    return values


def widen(values, length):
    segments, count = values.shape[0], values.shape[1]
    return jnp.broadcast_to(values.astype(jnp.float32)[:, :, None, :], (segments, count, ROWS, length))


def on_line(traces, valid, panel_owner, panel_start):
    channels, windows_here, segments, length = traces.shape
    bins = length // 2
    groups = lax.axis_size("tm")
    place = lax.axis_index("tm")
    chunks = 8
    width = channels // chunks
    seg_count = windows_here * segments
    sample = jnp.arange(length, dtype=jnp.int32)
    bin_index = jnp.arange(bins, dtype=jnp.int32)
    angles = (sample[:, None] * bin_index[None, :] % length).astype(jnp.float32) * (2.0 * math.pi / length)
    cosine, sine = lax.optimization_barrier((jnp.cos(angles), jnp.sin(angles)))
    forward = jnp.concatenate([cosine, -sine], axis=1).astype(jnp.bfloat16)
    rows = traces.reshape(channels, seg_count, length)
    mask = valid.reshape(channels, seg_count).transpose(1, 0).astype(jnp.float32)[:, :, None]
    whitened = whiten_segments(rows, mask, forward, chunks)
    block_place = lax.axis_index("block")
    pieces = []
    for panel in range(NP):
        first = panel_start[panel]
        chunk_of = first // width
        candidate = lax.dynamic_slice_in_dim(
            lax.dynamic_index_in_dim(whitened, chunk_of, 0, keepdims=False), first - chunk_of * width, PP, 1
        )
        pieces.append(jnp.where(block_place == panel_owner[panel], candidate, 0).astype(candidate.dtype))
    sources = butterfly_sum(jnp.concatenate(pieces, axis=1), "block")
    source_count = sources.shape[1]
    per_group = source_count // groups
    half = source_count // 2
    first_half = place < groups // 2
    turned = jnp.concatenate(
        [sources[:, source_count - per_group:], sources[:, half:source_count - per_group]], axis=1
    )
    far = jnp.where(first_half, turned, sources[:, :half])
    near = jnp.where(first_half, sources[:, :half], turned)
    factor = 1.0 / math.sqrt(bins * seg_count * groups)
    weight = jnp.where(bin_index == 0, 1.0, 2.0).astype(jnp.float32)[:, None] * factor
    inverse = jnp.concatenate([weight * cosine.T, -weight * sine.T], axis=0)
    is_edge = jnp.logical_or(place == 0, place == groups - 1)
    order = jnp.concatenate([far, near[:, per_group:], near[:, :per_group]], axis=1)
    order_wide = widen(order, length)
    outs = []
    arrived = []
    returned = []
    for chunk in range(chunks):
        own = whitened[chunk]
        if chunk >= 3:
            own, _, _ = lax.optimization_barrier((own, arrived[chunk - 2], returned[chunk - 3]))
        elif chunk >= 2:
            own, _ = lax.optimization_barrier((own, arrived[chunk - 2]))
        part = cross_chunk(own, order_wide)
        far_part = part[:half]
        near_part = jnp.concatenate([part[source_count - per_group:], part[half:source_count - per_group]], axis=0)
        edge_out = part[:source_count - per_group].astype(jnp.bfloat16)
        if arrived:
            edge_out, _ = lax.optimization_barrier((edge_out, arrived[-1]))
        edge_in = edge_first(edge_out, groups)
        arrived.append(edge_in)
        far_total = far_part + edge_in[:half].astype(jnp.float32)
        got = lax.ppermute(far_total.astype(jnp.bfloat16), "tm", [(1, 2), (2, 1)]).astype(jnp.float32)
        low = near_part[:per_group] + got[:per_group]
        high = near_part[per_group:] + edge_in[half:].astype(jnp.float32) + got[per_group:]
        back = lax.ppermute(low, "tm", [(1, 0), (2, 3)])
        returned.append(back)
        final = jnp.where(is_edge, near_part[:per_group] + back, high)
        outs.append(jnp.dot(final, inverse, precision=lax.Precision.HIGH))
    return jnp.concatenate(outs, axis=1)


def solution(mesh):
    in_specs = (P("block", "tm", None, None), P("block", "tm", None), P(), P())
    out_specs = P("tm", "block", None)
    body = on_line if mesh.shape["tm"] == 4 else on_device
    return jax.shard_map(
        body, mesh=mesh, in_specs=in_specs, out_specs=out_specs, check_vma=False
    )
```

```python
import math

import jax
import jax.numpy as jnp
from jax import lax
from jax.sharding import PartitionSpec as P
from jax.experimental import pallas as pl
from jax.experimental.pallas import tpu as pltpu

PP = 4
NP = 4


def spread(value, axis, source):
    kept = jnp.where(lax.axis_index(axis) == source, value, 0).astype(value.dtype)
    return lax.psum(kept, axis)


def forward_table(length):
    sample = jnp.arange(length, dtype=jnp.int32)
    bin_index = jnp.arange(length // 2, dtype=jnp.int32)
    angles = (sample[:, None] * bin_index[None, :] % length).astype(jnp.float32) * (
        2.0 * math.pi / length
    )
    return jnp.concatenate([jnp.cos(angles), -jnp.sin(angles)], axis=1).astype(jnp.bfloat16)


def inverse_table(length, factor):
    bin_index = jnp.arange(length // 2, dtype=jnp.int32)
    lag_index = jnp.arange(length, dtype=jnp.int32)
    angles = (bin_index[:, None] * lag_index[None, :] % length).astype(jnp.float32) * (
        2.0 * math.pi / length
    )
    weight = jnp.where(bin_index == 0, 1.0, 2.0).astype(jnp.float32)[:, None] * factor
    return jnp.concatenate([weight * jnp.cos(angles), -weight * jnp.sin(angles)], axis=0)


def whiten(segment_rows, valid_mask, forward):
    spectrum = jnp.dot(segment_rows, forward, preferred_element_type=jnp.float32)
    energy = jnp.mean(spectrum * spectrum, axis=1, keepdims=True)
    return (spectrum * lax.rsqrt(energy + 1e-06) * valid_mask[:, None].astype(jnp.float32)).astype(
        jnp.bfloat16
    )


def spectra_rows(segment_rows, valid_mask, forward):
    return whiten(segment_rows, valid_mask, forward)


def correlate(left, right):
    bins = left.shape[-1] // 2
    left_both = jnp.concatenate([left[..., :bins], left[..., bins:]], axis=1)
    right_both = jnp.concatenate([right[..., :bins], right[..., bins:]], axis=1)
    right_turn = jnp.concatenate([right[..., bins:], -right[..., :bins]], axis=1)
    real_part = jnp.einsum(
        "jmk,imk->jik", left_both, right_both, preferred_element_type=jnp.float32
    )
    imag_part = jnp.einsum(
        "jmk,imk->jik", left_both, right_turn, preferred_element_type=jnp.float32
    )
    return jnp.concatenate([real_part, imag_part], axis=-1)


def fetch_panel(whitened, panel_root, panel_first):
    candidate = lax.dynamic_slice_in_dim(whitened, panel_first, PP, 0)
    return spread(candidate, "block", panel_root)


def on_device(traces, valid, panel_owner, panel_start):
    channels, windows_here, segments, length = traces.shape
    bins = length // 2
    forward = forward_table(length)
    whitened = spectra_rows(
        traces.reshape(channels * windows_here * segments, length),
        valid.reshape(channels * windows_here * segments),
        forward,
    )
    whitened = whitened.reshape(channels, windows_here, segments, 2 * bins)
    pieces = []
    for panel in range(NP):
        pieces.append(fetch_panel(whitened, panel_owner[panel], panel_start[panel]))
    sources = jnp.concatenate(pieces, axis=0)
    groups = lax.axis_size("tm")
    inverse = inverse_table(length, 1.0 / math.sqrt(bins * windows_here * segments * groups))
    source_count = sources.shape[0]
    own_rows = whitened.reshape(channels, windows_here * segments, 2 * bins)
    source_rows = sources.reshape(source_count, windows_here * segments, 2 * bins)
    stacked = lax.psum_scatter(
        correlate(source_rows, own_rows), "tm", scatter_dimension=0, tiled=True
    )
    return jnp.dot(stacked, inverse, precision=lax.Precision.HIGHEST)


def edge_first(values, groups):
    return lax.ppermute(values, "tm", [(0, 1), (groups - 1, groups - 2)])


def whiten_kernel(rows_ref, forward_ref, mask_ref, out_ref):
    spectrum = jnp.dot(rows_ref[...], forward_ref[...], preferred_element_type=jnp.float32)
    energy = jnp.mean(spectrum * spectrum, axis=1, keepdims=True)
    scaled = spectrum * lax.rsqrt(energy + 1e-06) * mask_ref[...]
    out_ref[...] = scaled.astype(jnp.bfloat16).reshape(out_ref.shape)


def whiten_segments(rows, mask, forward, chunks):
    segments, channels, length = rows.shape
    width = channels // chunks
    return pl.pallas_call(
        whiten_kernel,
        grid=(segments,),
        in_specs=[
            pl.BlockSpec((None, channels, length), lambda m: (m, 0, 0)),
            pl.BlockSpec((length, length), lambda m: (0, 0)),
            pl.BlockSpec((None, channels, 1), lambda m: (m, 0, 0)),
        ],
        out_specs=pl.BlockSpec((chunks, None, width, length), lambda m: (0, m, 0, 0)),
        out_shape=jax.ShapeDtypeStruct((chunks, segments, width, length), jnp.bfloat16),
    )(rows, forward, mask)


LANES = 128
ROWS = 8


def cross_kernel(own_ref, src_ref, out_ref):
    segments = own_ref.shape[0]
    sources = src_ref.shape[1]
    bins = own_ref.shape[-1] // 2

    def tile_body(index, carry):
        half = index // (bins // LANES)
        tile = index % (bins // LANES)
        rows = pl.ds(pl.multiple_of(half * ROWS, ROWS), ROWS)
        re_lanes = pl.ds(pl.multiple_of(tile * LANES, LANES), LANES)
        im_lanes = pl.ds(pl.multiple_of(bins + tile * LANES, LANES), LANES)

        def step(m, acc):
            wr = own_ref[m, rows, re_lanes].astype(jnp.float32)
            wi = own_ref[m, rows, im_lanes].astype(jnp.float32)
            out = []
            for j in range(sources):
                sr = src_ref[m, j, :, re_lanes]
                si = src_ref[m, j, :, im_lanes]
                out.append(acc[2 * j] + (wr * sr + wi * si))
                out.append(acc[2 * j + 1] + (wi * sr - wr * si))
            return tuple(out)

        acc = tuple(jnp.zeros((ROWS, LANES), jnp.float32) for _ in range(2 * sources))
        acc = lax.fori_loop(0, segments, step, acc)
        for j in range(sources):
            out_ref[j, rows, re_lanes] = acc[2 * j]
            out_ref[j, rows, im_lanes] = acc[2 * j + 1]
        return carry

    lax.fori_loop(0, (own_ref.shape[1] // ROWS) * (bins // LANES), tile_body, 0)


def cross_chunk(own, src):
    segments, width, length = own.shape
    sources = src.shape[1]
    step_rows = 2 * ROWS
    return pl.pallas_call(
        cross_kernel,
        grid=(width // step_rows,),
        in_specs=[
            pl.BlockSpec((segments, step_rows, length), lambda i: (0, i, 0)),
            pl.BlockSpec((segments, sources, ROWS, length), lambda i: (0, 0, 0, 0)),
        ],
        out_specs=pl.BlockSpec((sources, step_rows, length), lambda i: (0, i, 0)),
        out_shape=jax.ShapeDtypeStruct((sources, width, length), jnp.float32),
    )(own, src)


def butterfly_sum(values, axis):
    count = lax.axis_size(axis)
    step = 1
    while step < count:
        values = values + lax.ppermute(values, axis, [(b, b ^ step) for b in range(count)])
        step *= 2
    return values


def widen(values, length):
    segments, count = values.shape[0], values.shape[1]
    return jnp.broadcast_to(values.astype(jnp.float32)[:, :, None, :], (segments, count, ROWS, length))


def on_line(traces, valid, panel_owner, panel_start):
    channels, windows_here, segments, length = traces.shape
    bins = length // 2
    groups = lax.axis_size("tm")
    place = lax.axis_index("tm")
    chunks = 8
    width = channels // chunks
    seg_count = windows_here * segments
    sample = jnp.arange(length, dtype=jnp.int32)
    bin_index = jnp.arange(bins, dtype=jnp.int32)
    angles = (sample[:, None] * bin_index[None, :] % length).astype(jnp.float32) * (2.0 * math.pi / length)
    cosine, sine = lax.optimization_barrier((jnp.cos(angles), jnp.sin(angles)))
    forward = jnp.concatenate([cosine, -sine], axis=1).astype(jnp.bfloat16)
    rows = traces.reshape(channels, seg_count, length).transpose(1, 0, 2)
    mask = valid.reshape(channels, seg_count).transpose(1, 0).astype(jnp.float32)[:, :, None]
    whitened = whiten_segments(rows, mask, forward, chunks)
    block_place = lax.axis_index("block")
    pieces = []
    for panel in range(NP):
        first = panel_start[panel]
        chunk_of = first // width
        candidate = lax.dynamic_slice_in_dim(
            lax.dynamic_index_in_dim(whitened, chunk_of, 0, keepdims=False), first - chunk_of * width, PP, 1
        )
        pieces.append(jnp.where(block_place == panel_owner[panel], candidate, 0).astype(candidate.dtype))
    sources = butterfly_sum(jnp.concatenate(pieces, axis=1), "block")
    source_count = sources.shape[1]
    per_group = source_count // groups
    half = source_count // 2
    first_half = place < groups // 2
    turned = jnp.concatenate(
        [sources[:, source_count - per_group:], sources[:, half:source_count - per_group]], axis=1
    )
    far = jnp.where(first_half, turned, sources[:, :half])
    near = jnp.where(first_half, sources[:, :half], turned)
    factor = 1.0 / math.sqrt(bins * seg_count * groups)
    weight = jnp.where(bin_index == 0, 1.0, 2.0).astype(jnp.float32)[:, None] * factor
    inverse = jnp.concatenate([weight * cosine.T, -weight * sine.T], axis=0)
    is_edge = jnp.logical_or(place == 0, place == groups - 1)
    order = jnp.concatenate([far, near[:, per_group:], near[:, :per_group]], axis=1)
    order_wide = widen(order, length)
    outs = []
    arrived = []
    returned = []
    for chunk in range(chunks):
        own = whitened[chunk]
        if chunk >= 3:
            own, _, _ = lax.optimization_barrier((own, arrived[chunk - 2], returned[chunk - 3]))
        elif chunk >= 2:
            own, _ = lax.optimization_barrier((own, arrived[chunk - 2]))
        part = cross_chunk(own, order_wide)
        far_part = part[:half]
        near_part = jnp.concatenate([part[source_count - per_group:], part[half:source_count - per_group]], axis=0)
        edge_out = part[:source_count - per_group].astype(jnp.bfloat16)
        if arrived:
            edge_out, _ = lax.optimization_barrier((edge_out, arrived[-1]))
        edge_in = edge_first(edge_out, groups)
        arrived.append(edge_in)
        far_total = far_part + edge_in[:half].astype(jnp.float32)
        got = lax.ppermute(far_total.astype(jnp.bfloat16), "tm", [(1, 2), (2, 1)]).astype(jnp.float32)
        low = near_part[:per_group] + got[:per_group]
        high = near_part[per_group:] + edge_in[half:].astype(jnp.float32) + got[per_group:]
        back = lax.ppermute(low, "tm", [(1, 0), (2, 3)])
        returned.append(back)
        final = jnp.where(is_edge, near_part[:per_group] + back, high)
        outs.append(jnp.dot(final, inverse, preferred_element_type=jnp.float32))
    return jnp.concatenate(outs, axis=1)


def solution(mesh):
    in_specs = (P("block", "tm", None, None), P("block", "tm", None), P(), P())
    out_specs = P("tm", "block", None)
    body = on_line if mesh.shape["tm"] == 4 else on_device
    return jax.shard_map(
        body, mesh=mesh, in_specs=in_specs, out_specs=out_specs, check_vma=False
    )
```
